512 devices in a mesh: sub: 32 (over x_lo, z, core), grp: 16 (over x_hi, y).
Axes of the slice: x: 4 (x_hi: 2, x_lo: 2; x = x_hi * 2 + x_lo), y: 8, z: 8, core: 2. Of those that a mesh axis runs over, the one named last changes fastest.
Arguments:
- deflation: bfloat16 [32, 3, 512, 128, 128], P(None, None, 'sub', 'grp'), may hold values from -10 to 10, as said below
- stiffness: bfloat16 [4, 512, 128, 128], P(None, 'sub', 'grp'), may hold values from 0.02 to 40, as said below
- depths: int32 [512], P(('sub', 'grp')), may hold values from 1 to 128, 49152 in all
Outputs:
- coarse_rows: float32 [32, 16, 32, 96], P('sub')
The draws below stay inside these ranges and needn't reach their ends.
Inputs may be any that keep to these rules, and one draw needn't show every extreme that they name: `deflation`: entries of order one. `stiffness`: positive coefficients. `depths`: the deepest subdomain has all 128 cells live.
All inputs are finite; a program needn't handle non-finite values. No bound on the sum of `depths` on one device may be relied on, other than what follows from the above.
Results may differ from the reference program's by a relative error of at most 0.0003.
Values may be sent and summed in bfloat16 or wider, within the bound.
No kernel may reach another device: no remote copies, remote signals or barrier semaphores. Data moves between devices by JAX's collectives and lax.ppermute only.
A program may use at most 128 MiB of HBM per device.

```python
import math
import jax
import jax.numpy as jnp
import numpy as np
from jax import lax

K = 32
CX = 16
CY = 8
CZ = 128
NX = 512
NY = 128
SUBDOMAINS = 512
N_SUB = 32
N_GRP = 16


def draw_deflation(key, part):
    key_noise, key_shared, key_signs = jax.random.split(key, 3)
    noise_part = jnp.clip(jax.random.normal(key_noise, (K, 3, NX, NY, CZ), jnp.float32), -6.0, 6.0)
    shared = jax.random.uniform(key_shared, (1, 1, NX, NY, CZ), jnp.float32, 0.5, 2.0)
    vector_signs = jax.random.uniform(key_signs, (K, 3, 1, 1, 1), jnp.float32, -1.0, 1.0)
    return (noise_part + 0.8 * shared * vector_signs).astype(jnp.bfloat16)


def draw_stiffness(key, part):
    key_region, key_cell = jax.random.split(key)
    region = jnp.exp(jax.random.uniform(key_region, (4, NX // CX, 1, NY // CY, 1, 1), jnp.float32, math.log(0.1), math.log(10.0)))
    region = jnp.broadcast_to(region, (4, NX // CX, CX, NY // CY, CY, CZ)).reshape(4, NX, NY, CZ)
    cell_factor = jnp.exp(jax.random.uniform(key_cell, (4, NX, NY, CZ), jnp.float32, math.log(0.5), math.log(2.0)))
    return (region * cell_factor).astype(jnp.bfloat16)


def split_up(count, total, reach, skew):
    loads = [(1 << 20) // math.isqrt(rank ** skew) + 1 for rank in range(2, count + 1)]
    spare, holding = total - reach - (count - 1), [1] * (count - 1)
    while spare > 0:
        movable = [i for i in range(count - 1) if holding[i] < reach]
        pool, left = sum([loads[i] for i in movable]), spare
        for i in movable:
            more = min(reach - holding[i], max(1, left * loads[i] // pool), spare)
            holding[i] = holding[i] + more
            spare = spare - more
    return np.array([reach] + holding)


def ragged_sizes(rng, count, total, most, skew):
    if count == 2:
        one = jax.random.randint(rng, (), max(1, total - most), min(most, total - 1) + 1)
        return jnp.stack([one, total - one])
    lengths = jnp.asarray(split_up(count, total, most, skew), jnp.int32)
    couples = (count - 1) // 2
    source_of, receiver = lengths[1:1 + 2 * couples:2], lengths[2:2 + 2 * couples:2]
    room = jnp.minimum(source_of - 1, most - receiver)
    moved = jax.random.randint(jax.random.fold_in(rng, 1), (couples,), 0, 1 << 20) % (room + 1)
    lengths = lengths.at[1:1 + 2 * couples:2].set(source_of - moved).at[2:2 + 2 * couples:2].set(receiver + moved)
    return lengths[jax.random.permutation(jax.random.fold_in(rng, 2), count)]


def setup_inputs(seed: int = 0) -> dict:
    streams_of = jax.random.split(jax.random.key(seed), 4)
    return {
        "deflation": draw_deflation(jax.random.fold_in(streams_of[3], 71), 0),
        "stiffness": draw_stiffness(jax.random.fold_in(streams_of[3], 71), 0),
        "depths": ragged_sizes(streams_of[2], SUBDOMAINS, SUBDOMAINS * CZ * 3 // 4, CZ, 2).astype(jnp.int32),
    }


def gram_of(left_side, right_side):
    count = left_side.shape[0]
    return jnp.dot(left_side.reshape(count, -1), right_side.reshape(count, -1).T, preferred_element_type=jnp.float32)


def weighted(weight, values):
    return (weight.astype(jnp.float32) * values.astype(jnp.float32)).astype(jnp.bfloat16)


def differences(values, dim_index):
    widened = values.astype(jnp.float32)
    length = widened.shape[dim_index]
    following = jnp.concatenate([lax.slice_in_dim(widened, 1, length, axis=dim_index), jnp.zeros_like(lax.slice_in_dim(widened, 0, 1, axis=dim_index))], axis=dim_index)
    return (widened - following).astype(jnp.bfloat16)


def local_terms(live_field, coefficients):
    accumulated = gram_of(live_field, weighted(coefficients[0], live_field))
    for entry in range(3):
        stepped = differences(live_field, entry + 2)
        accumulated = accumulated + gram_of(stepped, weighted(coefficients[entry + 1], stepped))
    return accumulated


def reference(deflation, stiffness, depths):
    normalizer = 1.0 / (24.0 * CX * CY * CZ)
    anchor = jnp.zeros((), jnp.int32)

    def live_block(slab, column):
        starts = (anchor, anchor, (slab * CX).astype(jnp.int32), (column * CY).astype(jnp.int32), anchor)
        sub_block = lax.dynamic_slice(deflation, starts, (K, 3, CX, CY, CZ))
        depth = depths[slab * N_GRP + column]
        live_mask = (jnp.arange(CZ, dtype=jnp.int32) < depth).astype(jnp.bfloat16)
        return sub_block * live_mask

    def coeff_block(slab, column):
        starts = (anchor, (slab * CX).astype(jnp.int32), (column * CY).astype(jnp.int32), anchor)
        return lax.dynamic_slice(stiffness, starts, (4, CX, CY, CZ))

    def subdomain_rows(index):
        slab = index // N_GRP
        column = index % N_GRP
        live_field = live_block(slab, column)
        coefficients = coeff_block(slab, column)
        diagonal_block = local_terms(live_field, coefficients)
        lower_x = coeff_block(jnp.maximum(slab - 1, 0), column)[1, CX - 1]
        weight_low_x = jnp.where(slab > 0, lower_x, jnp.zeros_like(lower_x))
        bottom_x = live_field[:, :, 0]
        diagonal_block = diagonal_block + gram_of(bottom_x, weighted(weight_low_x, bottom_x))
        lower_y = coeff_block(slab, jnp.maximum(column - 1, 0))[2, :, CY - 1]
        weight_low_y = jnp.where(column > 0, lower_y, jnp.zeros_like(lower_y))
        bottom_y = live_field[:, :, :, 0]
        diagonal_block = diagonal_block + gram_of(bottom_y, weighted(weight_low_y, bottom_y))
        next_x = live_block(jnp.minimum(slab + 1, N_SUB - 1), column)[:, :, 0]
        next_x = jnp.where(slab + 1 < N_SUB, next_x, jnp.zeros_like(next_x))
        coupling_x = -gram_of(weighted(coefficients[1, CX - 1], live_field[:, :, CX - 1]), next_x)
        next_y = live_block(slab, jnp.minimum(column + 1, N_GRP - 1))[:, :, :, 0]
        next_y = jnp.where(column + 1 < N_GRP, next_y, jnp.zeros_like(next_y))
        coupling_y = -gram_of(weighted(coefficients[2, :, CY - 1], live_field[:, :, :, CY - 1]), next_y)
        return normalizer * jnp.concatenate([diagonal_block, coupling_x, coupling_y], axis=1)

    all_rows = lax.map(subdomain_rows, jnp.arange(N_SUB * N_GRP, dtype=jnp.int32))
    return all_rows.reshape(N_SUB, N_GRP, K, 3 * K)
```

```python
import jax
import jax.numpy as jnp
from jax import lax
from jax.experimental import pallas as pl
from jax.experimental.pallas import tpu as pltpu
from jax.sharding import PartitionSpec as P


def from_behind(x, axis, by):
    length = lax.axis_size(axis)
    pairs = [(i, i + by) for i in range(length) if 0 <= i + by < length]
    return lax.ppermute(x, axis, pairs)


def gram_of(left_side, right_side):
    count = left_side.shape[0]
    return jnp.dot(
        left_side.reshape(count, -1),
        right_side.reshape(count, -1).T,
        preferred_element_type=jnp.float32,
    )


def weighted(weight, values):
    return (weight.astype(jnp.float32) * values.astype(jnp.float32)).astype(jnp.bfloat16)


def local_kernel(live_ref, coeff_ref, out_ref):
    comps, rows, count, width = live_ref.shape
    lane = lax.broadcasted_iota(jnp.int32, (count, width), 1)
    last_z = (lane & 127) == 127
    zero_slab = jnp.zeros((count, 128), jnp.float32)

    def weight(entry, row):
        return coeff_ref[entry, pl.ds(row, 1), :]

    def body(row, acc):
        has_next = row < rows - 1
        following_row = jnp.minimum(row + 1, rows - 1)
        w_mass = weight(0, row)
        w_x = weight(1, row)
        w_y = weight(2, row)
        w_z = weight(3, row)
        lefts, rights = [], []
        for comp in range(comps):
            live_b = live_ref[comp, row]
            live = live_b.astype(jnp.float32)
            next_x = live_ref[comp, following_row].astype(jnp.float32)
            next_x = jnp.where(has_next, next_x, 0.0)
            next_y = jnp.concatenate([live[:, 128:], zero_slab], axis=1)
            next_z = jnp.where(last_z, 0.0, pltpu.roll(live, width - 1, 1))
            step_x = (live - next_x).astype(jnp.bfloat16)
            step_y = (live - next_y).astype(jnp.bfloat16)
            step_z = (live - next_z).astype(jnp.bfloat16)
            lefts += [live_b, step_x, step_y, step_z]
            rights += [
                (w_mass * live).astype(jnp.bfloat16),
                (w_x * step_x.astype(jnp.float32)).astype(jnp.bfloat16),
                (w_y * step_y.astype(jnp.float32)).astype(jnp.bfloat16),
                (w_z * step_z.astype(jnp.float32)).astype(jnp.bfloat16),
            ]
        left = jnp.concatenate(lefts, axis=1)
        right = jnp.concatenate(rights, axis=1)
        return acc + lax.dot_general(
            left, right, (((1,), (1,)), ((), ())), preferred_element_type=jnp.float32
        )

    acc = lax.fori_loop(0, rows, body, jnp.zeros((count, count), jnp.float32))
    out_ref[...] = acc


def local_terms(live_field, coefficients):
    count, comps, rows, cols, depth = live_field.shape
    live_t = jnp.transpose(live_field, (1, 2, 0, 3, 4)).reshape(comps, rows, count, cols * depth)
    coeff_t = coefficients.astype(jnp.float32).reshape(4, rows, cols * depth)
    return pl.pallas_call(
        local_kernel,
        out_shape=jax.ShapeDtypeStruct((count, count), jnp.float32),
        in_specs=[pl.BlockSpec(memory_space=pltpu.VMEM)] * 2,
        out_specs=pl.BlockSpec(memory_space=pltpu.VMEM),
        cost_estimate=pl.CostEstimate(
            flops=2 * 4 * count * count * live_field.size // count,
            bytes_accessed=live_t.size * 2 + coeff_t.size * 4,
            transcendentals=0,
        ),
    )(live_t, coeff_t)


def shards(deflation, stiffness, depths):
    cell_count = deflation.shape[2] * deflation.shape[3] * deflation.shape[4]
    normalizer = 1.0 / (24.0 * cell_count)
    live_mask = (lax.iota(jnp.int32, deflation.shape[4]) < depths[0]).astype(jnp.bfloat16)
    live_field = deflation * live_mask
    diagonal_block = local_terms(live_field, stiffness)
    top_x = live_field[:, :, -1]
    bottom_x = live_field[:, :, 0]
    weight_top_x = stiffness[1, -1]
    next_x = from_behind(bottom_x, "sub", -1)
    coupling_x = -gram_of(weighted(weight_top_x, top_x), next_x)
    face_term = gram_of(next_x, weighted(weight_top_x, next_x))
    lower_x = from_behind(face_term, "sub", 1)
    diagonal_block = diagonal_block + lower_x
    bottom_y = live_field[:, :, :, 0]
    weight_top_y = stiffness[2, :, -1]
    next_y = from_behind(bottom_y, "grp", -1)
    weight_low_y = from_behind(weight_top_y, "grp", 1)
    diagonal_block = diagonal_block + gram_of(bottom_y, weighted(weight_low_y, bottom_y))
    coupling_y = -gram_of(weighted(weight_top_y, live_field[:, :, :, -1]), next_y)
    row_block = normalizer * jnp.concatenate([diagonal_block, coupling_x, coupling_y], axis=1)
    return lax.all_gather(row_block[None, None], "grp", axis=1, tiled=True)


def solution(mesh):
    in_specs = (P(None, None, "sub", "grp", None), P(None, "sub", "grp", None), P(("sub", "grp")))
    out_specs = P("sub", None, None, None)
    return jax.shard_map(shards, mesh=mesh, in_specs=in_specs, out_specs=out_specs, check_vma=False)
```

```python
import jax
import jax.numpy as jnp
from jax import lax
from jax.experimental import pallas as pl
from jax.experimental.pallas import tpu as pltpu
from jax.sharding import PartitionSpec as P


def from_behind(x, axis, by):
    length = lax.axis_size(axis)
    pairs = [(i, i + by) for i in range(length) if 0 <= i + by < length]
    return lax.ppermute(x, axis, pairs)


def gram_of(left_side, right_side):
    count = left_side.shape[0]
    return jnp.dot(
        left_side.reshape(count, -1),
        right_side.reshape(count, -1).T,
        preferred_element_type=jnp.float32,
    )


def weighted(weight, values):
    return (weight.astype(jnp.float32) * values.astype(jnp.float32)).astype(jnp.bfloat16)


def local_kernel(live_ref, coeff_ref, out_ref):
    comps, rows, count, width = live_ref.shape
    lane = lax.broadcasted_iota(jnp.int32, (count, width), 1)
    last_z = (lane & 127) == 127
    zero_slab = jnp.zeros((count, 128), jnp.float32)

    def weight(entry, row):
        return coeff_ref[entry, pl.ds(row, 1), :]

    def body(row, acc):
        has_next = row < rows - 1
        following_row = jnp.minimum(row + 1, rows - 1)
        w_mass = weight(0, row)
        w_x = weight(1, row)
        w_y = weight(2, row)
        w_z = weight(3, row)
        lefts, rights = [], []
        for comp in range(comps):
            live_b = live_ref[comp, row]
            live = live_b.astype(jnp.float32)
            next_x = live_ref[comp, following_row].astype(jnp.float32)
            next_x = jnp.where(has_next, next_x, 0.0)
            next_y = jnp.concatenate([live[:, 128:], zero_slab], axis=1)
            next_z = jnp.where(last_z, 0.0, pltpu.roll(live, width - 1, 1))
            step_x = (live - next_x).astype(jnp.bfloat16)
            step_y = (live - next_y).astype(jnp.bfloat16)
            step_z = (live - next_z).astype(jnp.bfloat16)
            lefts += [live_b, step_x, step_y, step_z]
            rights += [
                (w_mass * live).astype(jnp.bfloat16),
                (w_x * step_x.astype(jnp.float32)).astype(jnp.bfloat16),
                (w_y * step_y.astype(jnp.float32)).astype(jnp.bfloat16),
                (w_z * step_z.astype(jnp.float32)).astype(jnp.bfloat16),
            ]
        left = jnp.concatenate(lefts, axis=1)
        right = jnp.concatenate(rights, axis=1)
        return acc + lax.dot_general(
            left, right, (((1,), (1,)), ((), ())), preferred_element_type=jnp.float32
        )

    acc = lax.fori_loop(0, rows, body, jnp.zeros((count, count), jnp.float32))
    out_ref[...] = acc


def local_terms(live_field, coefficients):
    count, comps, rows, cols, depth = live_field.shape
    live_t = jnp.transpose(live_field, (1, 2, 0, 3, 4)).reshape(comps, rows, count, cols * depth)
    coeff_t = coefficients.astype(jnp.float32).reshape(4, rows, cols * depth)
    return pl.pallas_call(
        local_kernel,
        out_shape=jax.ShapeDtypeStruct((count, count), jnp.float32),
        in_specs=[pl.BlockSpec(memory_space=pltpu.VMEM)] * 2,
        out_specs=pl.BlockSpec(memory_space=pltpu.VMEM),
        cost_estimate=pl.CostEstimate(
            flops=2 * 4 * count * count * live_field.size // count,
            bytes_accessed=live_t.size * 2 + coeff_t.size * 4,
            transcendentals=0,
        ),
    )(live_t, coeff_t)


def shards(deflation, stiffness, depths):
    cell_count = deflation.shape[2] * deflation.shape[3] * deflation.shape[4]
    normalizer = 1.0 / (24.0 * cell_count)
    live_mask = (lax.iota(jnp.int32, deflation.shape[4]) < depths[0]).astype(jnp.bfloat16)
    live_field = deflation * live_mask
    diagonal_block = local_terms(live_field, stiffness)
    top_x = live_field[:, :, -1]
    bottom_x = live_field[:, :, 0]
    weight_top_x = stiffness[1, -1]
    next_x = from_behind(bottom_x, "sub", -1)
    coupling_x = -gram_of(weighted(weight_top_x, top_x), next_x)
    face_term = gram_of(next_x, weighted(weight_top_x, next_x))
    lower_x = from_behind(face_term, "sub", 1)
    diagonal_block = diagonal_block + lower_x
    bottom_y = live_field[:, :, :, 0]
    weight_top_y = stiffness[2, :, -1]
    next_y = from_behind(bottom_y, "grp", -1)
    weight_low_y = from_behind(weight_top_y, "grp", 1)
    diagonal_block = diagonal_block + gram_of(bottom_y, weighted(weight_low_y, bottom_y))
    coupling_y = -gram_of(weighted(weight_top_y, live_field[:, :, :, -1]), next_y)
    row_block = normalizer * jnp.concatenate([diagonal_block, coupling_x, coupling_y], axis=1)
    groups = lax.axis_size("grp")
    copies = jnp.broadcast_to(row_block[None, None], (1, groups) + row_block.shape)
    return lax.all_to_all(copies, "grp", 1, 1, tiled=True)


def solution(mesh):
    in_specs = (P(None, None, "sub", "grp", None), P(None, "sub", "grp", None), P(("sub", "grp")))
    out_specs = P("sub", None, None, None)
    return jax.shard_map(shards, mesh=mesh, in_specs=in_specs, out_specs=out_specs, check_vma=False)
```

```python
import jax
import jax.numpy as jnp
from jax import lax
from jax.experimental import pallas as pl
from jax.experimental.pallas import tpu as pltpu
from jax.sharding import PartitionSpec as P


def from_behind(x, axis, by):
    length = lax.axis_size(axis)
    pairs = [(i, i + by) for i in range(length) if 0 <= i + by < length]
    return lax.ppermute(x, axis, pairs)


def gram_of(left_side, right_side):
    count = left_side.shape[0]
    return jnp.dot(
        left_side.reshape(count, -1),
        right_side.reshape(count, -1).T,
        preferred_element_type=jnp.float32,
    )


def weighted(weight, values):
    return (weight.astype(jnp.float32) * values.astype(jnp.float32)).astype(jnp.bfloat16)


def local_kernel(depth_ref, defl_ref, coeff_ref, out_ref):
    count, comps, rows, cols, depth = defl_ref.shape
    lane = lax.broadcasted_iota(jnp.int32, (count, depth), 1)
    live_mask = (lane < depth_ref[0]).astype(jnp.bfloat16)
    last_z = lane == depth - 1

    def slab(comp, row, col):
        return (defl_ref[:, comp, row, col, :] * live_mask).astype(jnp.float32)

    def weight(entry, row, col):
        return coeff_ref[entry, row, pl.ds(col, 1), :].astype(jnp.float32)

    def body(row, acc):
        has_next = row < rows - 1
        following_row = jnp.minimum(row + 1, rows - 1)
        for comp in range(comps):
            lefts, rights = [], []
            lives = [slab(comp, row, col) for col in range(cols)]
            for col in range(cols):
                live = lives[col]
                next_x = jnp.where(has_next, slab(comp, following_row, col), 0.0)
                next_y = lives[col + 1] if col + 1 < cols else jnp.zeros_like(live)
                next_z = jnp.where(last_z, 0.0, pltpu.roll(live, depth - 1, 1))
                step_x = (live - next_x).astype(jnp.bfloat16)
                step_y = (live - next_y).astype(jnp.bfloat16)
                step_z = (live - next_z).astype(jnp.bfloat16)
                lefts += [live.astype(jnp.bfloat16), step_x, step_y, step_z]
                rights += [
                    (weight(0, row, col) * live).astype(jnp.bfloat16),
                    (weight(1, row, col) * step_x.astype(jnp.float32)).astype(jnp.bfloat16),
                    (weight(2, row, col) * step_y.astype(jnp.float32)).astype(jnp.bfloat16),
                    (weight(3, row, col) * step_z.astype(jnp.float32)).astype(jnp.bfloat16),
                ]
            left = jnp.concatenate(lefts, axis=1)
            right = jnp.concatenate(rights, axis=1)
            acc = acc + lax.dot_general(
                left, right, (((1,), (1,)), ((), ())), preferred_element_type=jnp.float32
            )
        return acc

    acc = lax.fori_loop(0, rows, body, jnp.zeros((count, count), jnp.float32))
    out_ref[...] = acc


def local_terms(deflation, coefficients, depths):
    count = deflation.shape[0]
    return pl.pallas_call(
        local_kernel,
        out_shape=jax.ShapeDtypeStruct((count, count), jnp.float32),
        in_specs=[pl.BlockSpec(memory_space=pltpu.SMEM)] + [pl.BlockSpec(memory_space=pltpu.VMEM)] * 2,
        out_specs=pl.BlockSpec(memory_space=pltpu.VMEM),
        cost_estimate=pl.CostEstimate(
            flops=2 * 4 * count * deflation.size,
            bytes_accessed=deflation.size * 2 + coefficients.size * 2,
            transcendentals=0,
        ),
    )(depths, deflation, coefficients)


def shards(deflation, stiffness, depths):
    cell_count = deflation.shape[2] * deflation.shape[3] * deflation.shape[4]
    normalizer = 1.0 / (24.0 * cell_count)
    live_mask = (lax.iota(jnp.int32, deflation.shape[4]) < depths[0]).astype(jnp.bfloat16)
    live_field = deflation * live_mask
    diagonal_block = local_terms(deflation, stiffness, depths)
    top_x = live_field[:, :, -1]
    bottom_x = live_field[:, :, 0]
    weight_top_x = stiffness[1, -1]
    next_x = from_behind(bottom_x, "sub", -1)
    coupling_x = -gram_of(weighted(weight_top_x, top_x), next_x)
    face_term = gram_of(next_x, weighted(weight_top_x, next_x))
    lower_x = from_behind(face_term, "sub", 1)
    diagonal_block = diagonal_block + lower_x
    bottom_y = live_field[:, :, :, 0]
    weight_top_y = stiffness[2, :, -1]
    next_y = from_behind(bottom_y, "grp", -1)
    weight_low_y = from_behind(weight_top_y, "grp", 1)
    diagonal_block = diagonal_block + gram_of(bottom_y, weighted(weight_low_y, bottom_y))
    coupling_y = -gram_of(weighted(weight_top_y, live_field[:, :, :, -1]), next_y)
    row_block = normalizer * jnp.concatenate([diagonal_block, coupling_x, coupling_y], axis=1)
    groups = lax.axis_size("grp")
    copies = jnp.broadcast_to(row_block[None, None], (1, groups) + row_block.shape)
    return lax.all_to_all(copies, "grp", 1, 1, tiled=True)


def solution(mesh):
    in_specs = (P(None, None, "sub", "grp", None), P(None, "sub", "grp", None), P(("sub", "grp")))
    out_specs = P("sub", None, None, None)
    return jax.shard_map(shards, mesh=mesh, in_specs=in_specs, out_specs=out_specs, check_vma=False)
```

```python
import jax
import jax.numpy as jnp
from jax import lax
from jax.experimental import pallas as pl
from jax.experimental.pallas import tpu as pltpu
from jax.sharding import PartitionSpec as P


def from_behind(x, axis, by):
    length = lax.axis_size(axis)
    pairs = [(i, i + by) for i in range(length) if 0 <= i + by < length]
    return lax.ppermute(x, axis, pairs)


def gram_of(left_side, right_side):
    count = left_side.shape[0]
    return jnp.dot(
        left_side.reshape(count, -1),
        right_side.reshape(count, -1).T,
        preferred_element_type=jnp.float32,
    )


def weighted(weight, values):
    return (weight.astype(jnp.float32) * values.astype(jnp.float32)).astype(jnp.bfloat16)


def local_kernel(depth_ref, defl_ref, coeff_ref, out_ref):
    count, comps, rows, cols, depth = defl_ref.shape
    lane = lax.broadcasted_iota(jnp.int32, (count, depth), 1)
    live_mask = (lane < depth_ref[0]).astype(jnp.bfloat16)
    last_z = lane == depth - 1

    def slab(comp, row, col):
        return (defl_ref[:, comp, row, col, :] * live_mask).astype(jnp.float32)

    def weight(entry, row, col):
        return coeff_ref[entry, row, pl.ds(col, 1), :].astype(jnp.float32)

    def body(row, acc):
        has_next = row < rows - 1
        following_row = jnp.minimum(row + 1, rows - 1)
        for comp in range(comps):
            lefts, rights = [], []
            lives = [slab(comp, row, col) for col in range(cols)]
            for col in range(cols):
                live = lives[col]
                next_x = jnp.where(has_next, slab(comp, following_row, col), 0.0)
                next_y = lives[col + 1] if col + 1 < cols else jnp.zeros_like(live)
                next_z = jnp.where(last_z, 0.0, pltpu.roll(live, depth - 1, 1))
                step_x = (live - next_x).astype(jnp.bfloat16)
                step_y = (live - next_y).astype(jnp.bfloat16)
                step_z = (live - next_z).astype(jnp.bfloat16)
                lefts += [live.astype(jnp.bfloat16), step_x, step_y, step_z]
                rights += [
                    (weight(0, row, col) * live).astype(jnp.bfloat16),
                    (weight(1, row, col) * step_x.astype(jnp.float32)).astype(jnp.bfloat16),
                    (weight(2, row, col) * step_y.astype(jnp.float32)).astype(jnp.bfloat16),
                    (weight(3, row, col) * step_z.astype(jnp.float32)).astype(jnp.bfloat16),
                ]
            left = jnp.concatenate(lefts, axis=1)
            right = jnp.concatenate(rights, axis=1)
            acc = acc + lax.dot_general(
                left, right, (((1,), (1,)), ((), ())), preferred_element_type=jnp.float32
            )
        return acc

    acc = lax.fori_loop(0, rows, body, jnp.zeros((count, count), jnp.float32))
    out_ref[...] = acc


def local_terms(deflation, coefficients, depths):
    count = deflation.shape[0]
    return pl.pallas_call(
        local_kernel,
        out_shape=jax.ShapeDtypeStruct((count, count), jnp.float32),
        in_specs=[pl.BlockSpec(memory_space=pltpu.SMEM)] + [pl.BlockSpec(memory_space=pltpu.VMEM)] * 2,
        out_specs=pl.BlockSpec(memory_space=pltpu.VMEM),
        cost_estimate=pl.CostEstimate(
            flops=2 * 4 * count * deflation.size,
            bytes_accessed=deflation.size * 2 + coefficients.size * 2,
            transcendentals=0,
        ),
    )(depths, deflation, coefficients)


def shards(deflation, stiffness, depths):
    cell_count = deflation.shape[2] * deflation.shape[3] * deflation.shape[4]
    normalizer = 1.0 / (24.0 * cell_count)
    live_mask = (lax.iota(jnp.int32, deflation.shape[4]) < depths[0]).astype(jnp.bfloat16)
    bottom_x = deflation[:, :, 0] * live_mask
    bottom_y = deflation[:, :, :, 0] * live_mask
    weight_top_x = stiffness[1, -1]
    weight_top_y = stiffness[2, :, -1]
    next_x = from_behind(bottom_x, "sub", -1)
    weight_low_x = from_behind(weight_top_x, "sub", 1)
    next_y = from_behind(bottom_y, "grp", -1)
    weight_low_y = from_behind(weight_top_y, "grp", 1)
    diagonal_block = local_terms(deflation, stiffness, depths)
    top_x = deflation[:, :, -1] * live_mask
    top_y = deflation[:, :, :, -1] * live_mask
    coupling_x = -gram_of(weighted(weight_top_x, top_x), next_x)
    coupling_y = -gram_of(weighted(weight_top_y, top_y), next_y)
    diagonal_block = diagonal_block + gram_of(bottom_x, weighted(weight_low_x, bottom_x))
    diagonal_block = diagonal_block + gram_of(bottom_y, weighted(weight_low_y, bottom_y))
    row_block = normalizer * jnp.concatenate([diagonal_block, coupling_x, coupling_y], axis=1)
    groups = lax.axis_size("grp")
    copies = jnp.broadcast_to(row_block[None, None], (1, groups) + row_block.shape)
    return lax.all_to_all(copies, "grp", 1, 1, tiled=True)


def solution(mesh):
    in_specs = (P(None, None, "sub", "grp", None), P(None, "sub", "grp", None), P(("sub", "grp")))
    out_specs = P("sub", None, None, None)
    return jax.shard_map(shards, mesh=mesh, in_specs=in_specs, out_specs=out_specs, check_vma=False)
```

```python
import jax
import jax.numpy as jnp
from jax import lax
from jax.experimental import pallas as pl
from jax.experimental.pallas import tpu as pltpu
from jax.sharding import PartitionSpec as P


def from_behind(x, axis, by):
    length = lax.axis_size(axis)
    pairs = [(i, i + by) for i in range(length) if 0 <= i + by < length]
    return lax.ppermute(x, axis, pairs)


def gram_of(left_side, right_side):
    count = left_side.shape[0]
    return jnp.dot(
        left_side.reshape(count, -1),
        right_side.reshape(count, -1).T,
        preferred_element_type=jnp.float32,
    )


def weighted(weight, values):
    return (weight.astype(jnp.float32) * values.astype(jnp.float32)).astype(jnp.bfloat16)


def block_kernel(depth_ref, defl_ref, coeff_ref, out_ref, acc_ref):
    count, comps, rows, cols, depth = defl_ref.shape
    tall = count * cols
    lane = lax.broadcasted_iota(jnp.int32, (count, cols, depth), 2)
    sub = lax.broadcasted_iota(jnp.int32, (count, cols, depth), 1)
    live_mask = (lane < depth_ref[0]).astype(jnp.bfloat16)
    last_z = lane == depth - 1
    last_y = sub == cols - 1
    acc_ref[...] = jnp.zeros_like(acc_ref)

    def tiles(comp, row):
        return (defl_ref[:, comp, row] * live_mask).astype(jnp.float32)

    def body(row, carry):
        has_next = row < rows - 1
        following_row = jnp.minimum(row + 1, rows - 1)
        w = [coeff_ref[e, row].astype(jnp.float32)[None] for e in range(4)]
        lefts, rights = [], []
        for comp in range(comps):
            live = tiles(comp, row)
            next_x = jnp.where(has_next, tiles(comp, following_row), 0.0)
            next_y = jnp.where(last_y, 0.0, pltpu.roll(live, cols - 1, 1))
            next_z = jnp.where(last_z, 0.0, pltpu.roll(live, depth - 1, 2))
            step_x = (live - next_x).astype(jnp.bfloat16)
            step_y = (live - next_y).astype(jnp.bfloat16)
            step_z = (live - next_z).astype(jnp.bfloat16)
            lefts += [live.astype(jnp.bfloat16), step_x, step_y, step_z]
            rights += [
                (w[0] * live).astype(jnp.bfloat16),
                (w[1] * step_x.astype(jnp.float32)).astype(jnp.bfloat16),
                (w[2] * step_y.astype(jnp.float32)).astype(jnp.bfloat16),
                (w[3] * step_z.astype(jnp.float32)).astype(jnp.bfloat16),
            ]
        left = jnp.concatenate([v.reshape(tall, depth) for v in lefts], axis=1)
        right = jnp.concatenate([v.reshape(tall, depth) for v in rights], axis=1)
        acc_ref[...] += lax.dot_general(
            left, right, (((1,), (1,)), ((), ())), preferred_element_type=jnp.float32
        )
        return carry

    lax.fori_loop(0, rows, body, 0)
    r = lax.broadcasted_iota(jnp.int32, (tall, tall), 0)
    c = lax.broadcasted_iota(jnp.int32, (tall, tall), 1)
    same = (r & (cols - 1)) == (c & (cols - 1))
    kept = jnp.where(same, acc_ref[...], 0.0)
    out_ref[...] = kept.reshape(count, cols, tall).sum(axis=1)


def local_terms(deflation, coefficients, depths):
    count, comps, rows, cols, depth = deflation.shape
    tall = count * cols
    partial = pl.pallas_call(
        block_kernel,
        out_shape=jax.ShapeDtypeStruct((count, tall), jnp.float32),
        in_specs=[pl.BlockSpec(memory_space=pltpu.SMEM)] + [pl.BlockSpec(memory_space=pltpu.VMEM)] * 2,
        out_specs=pl.BlockSpec(memory_space=pltpu.VMEM),
        scratch_shapes=[pltpu.VMEM((tall, tall), jnp.float32)],
        cost_estimate=pl.CostEstimate(
            flops=2 * 4 * tall * tall * comps * rows * depth,
            bytes_accessed=deflation.size * 2 + coefficients.size * 2,
            transcendentals=0,
        ),
    )(depths, deflation, coefficients)
    return partial.reshape(count, count, cols).sum(axis=2)


def shards(deflation, stiffness, depths):
    cell_count = deflation.shape[2] * deflation.shape[3] * deflation.shape[4]
    normalizer = 1.0 / (24.0 * cell_count)
    live_mask = (lax.iota(jnp.int32, deflation.shape[4]) < depths[0]).astype(jnp.bfloat16)
    bottom_x = deflation[:, :, 0] * live_mask
    bottom_y = deflation[:, :, :, 0] * live_mask
    weight_top_x = stiffness[1, -1]
    weight_top_y = stiffness[2, :, -1]
    next_x = from_behind(bottom_x, "sub", -1)
    weight_low_x = from_behind(weight_top_x, "sub", 1)
    next_y = from_behind(bottom_y, "grp", -1)
    weight_low_y = from_behind(weight_top_y, "grp", 1)
    diagonal_block = local_terms(deflation, stiffness, depths)
    top_x = deflation[:, :, -1] * live_mask
    top_y = deflation[:, :, :, -1] * live_mask
    coupling_x = -gram_of(weighted(weight_top_x, top_x), next_x)
    coupling_y = -gram_of(weighted(weight_top_y, top_y), next_y)
    diagonal_block = diagonal_block + gram_of(bottom_x, weighted(weight_low_x, bottom_x))
    diagonal_block = diagonal_block + gram_of(bottom_y, weighted(weight_low_y, bottom_y))
    row_block = normalizer * jnp.concatenate([diagonal_block, coupling_x, coupling_y], axis=1)
    groups = lax.axis_size("grp")
    copies = jnp.broadcast_to(row_block[None, None], (1, groups) + row_block.shape)
    return lax.all_to_all(copies, "grp", 1, 1, tiled=True)


def solution(mesh):
    in_specs = (P(None, None, "sub", "grp", None), P(None, "sub", "grp", None), P(("sub", "grp")))
    out_specs = P("sub", None, None, None)
    return jax.shard_map(shards, mesh=mesh, in_specs=in_specs, out_specs=out_specs, check_vma=False)
```

```python
import jax
import jax.numpy as jnp
from jax import lax
from jax.experimental import pallas as pl
from jax.experimental.pallas import tpu as pltpu
from jax.sharding import PartitionSpec as P


def from_behind(x, axis, by):
    length = lax.axis_size(axis)
    pairs = [(i, i + by) for i in range(length) if 0 <= i + by < length]
    return lax.ppermute(x, axis, pairs)


def gram_of(left_side, right_side):
    count = left_side.shape[0]
    return jnp.dot(
        left_side.reshape(count, -1),
        right_side.reshape(count, -1).T,
        preferred_element_type=jnp.float32,
    )


def weighted(weight, values):
    return (weight.astype(jnp.float32) * values.astype(jnp.float32)).astype(jnp.bfloat16)


def block_kernel(depth_ref, defl_ref, coeff_ref, out_ref, acc_ref):
    count, comps, rows, cols, depth = defl_ref.shape
    tall = count * cols
    lane = lax.broadcasted_iota(jnp.int32, (count, cols, depth), 2)
    sub = lax.broadcasted_iota(jnp.int32, (count, cols, depth), 1)
    live_mask = (lane < depth_ref[0]).astype(jnp.bfloat16)
    last_z = lane == depth - 1
    last_y = sub == cols - 1
    acc_ref[...] = jnp.zeros_like(acc_ref)

    def body(row, carry):
        has_next = row < rows - 1
        following_row = jnp.minimum(row + 1, rows - 1)
        w = [coeff_ref[e, row][None] for e in range(4)]
        lefts, rights = [], []
        for comp in range(comps):
            live = defl_ref[:, comp, row] * live_mask
            next_x = jnp.where(has_next, defl_ref[:, comp, following_row] * live_mask, 0)
            wide = live.astype(jnp.float32)
            next_y = jnp.where(last_y, 0.0, pltpu.roll(wide, cols - 1, 1))
            next_z = jnp.where(last_z, 0, pltpu.roll(live, depth - 1, 2))
            step_x = live - next_x
            step_y = (wide - next_y).astype(jnp.bfloat16)
            step_z = live - next_z
            lefts += [live, step_x, step_y, step_z]
            rights += [w[0] * live, w[1] * step_x, w[2] * step_y, w[3] * step_z]
        left = jnp.concatenate([v.reshape(tall, depth) for v in lefts], axis=1)
        right = jnp.concatenate([v.reshape(tall, depth) for v in rights], axis=1)
        acc_ref[...] += lax.dot_general(
            left, right, (((1,), (1,)), ((), ())), preferred_element_type=jnp.float32
        )
        return carry

    lax.fori_loop(0, rows, body, 0)
    r = lax.broadcasted_iota(jnp.int32, (tall, tall), 0)
    c = lax.broadcasted_iota(jnp.int32, (tall, tall), 1)
    same = (r & (cols - 1)) == (c & (cols - 1))
    kept = jnp.where(same, acc_ref[...], 0.0)
    out_ref[...] = kept.reshape(count, cols, tall).sum(axis=1)


def local_terms(deflation, coefficients, depths):
    count, comps, rows, cols, depth = deflation.shape
    tall = count * cols
    partial = pl.pallas_call(
        block_kernel,
        out_shape=jax.ShapeDtypeStruct((count, tall), jnp.float32),
        in_specs=[pl.BlockSpec(memory_space=pltpu.SMEM)] + [pl.BlockSpec(memory_space=pltpu.VMEM)] * 2,
        out_specs=pl.BlockSpec(memory_space=pltpu.VMEM),
        scratch_shapes=[pltpu.VMEM((tall, tall), jnp.float32)],
        cost_estimate=pl.CostEstimate(
            flops=2 * 4 * tall * tall * comps * rows * depth,
            bytes_accessed=deflation.size * 2 + coefficients.size * 2,
            transcendentals=0,
        ),
    )(depths, deflation, coefficients)
    return partial.reshape(count, count, cols).sum(axis=2)


def shards(deflation, stiffness, depths):
    cell_count = deflation.shape[2] * deflation.shape[3] * deflation.shape[4]
    normalizer = 1.0 / (24.0 * cell_count)
    live_mask = (lax.iota(jnp.int32, deflation.shape[4]) < depths[0]).astype(jnp.bfloat16)
    bottom_x = deflation[:, :, 0] * live_mask
    bottom_y = deflation[:, :, :, 0] * live_mask
    weight_top_x = stiffness[1, -1]
    weight_top_y = stiffness[2, :, -1]
    next_x = from_behind(bottom_x, "sub", -1)
    weight_low_x = from_behind(weight_top_x, "sub", 1)
    next_y = from_behind(deflation[:, :, :, :2] * live_mask, "grp", -1)[:, :, :, 0]
    weight_low_y = from_behind(weight_top_y, "grp", 1)
    diagonal_block = local_terms(deflation, stiffness, depths)
    top_x = deflation[:, :, -1] * live_mask
    top_y = deflation[:, :, :, -1] * live_mask
    coupling_x = -gram_of(weighted(weight_top_x, top_x), next_x)
    coupling_y = -gram_of(weighted(weight_top_y, top_y), next_y)
    diagonal_block = diagonal_block + gram_of(bottom_x, weighted(weight_low_x, bottom_x))
    diagonal_block = diagonal_block + gram_of(bottom_y, weighted(weight_low_y, bottom_y))
    row_block = normalizer * jnp.concatenate([diagonal_block, coupling_x, coupling_y], axis=1)
    groups = lax.axis_size("grp")
    copies = jnp.broadcast_to(row_block[None, None], (1, groups) + row_block.shape)
    return lax.all_to_all(copies, "grp", 1, 1, tiled=True)


def solution(mesh):
    in_specs = (P(None, None, "sub", "grp", None), P(None, "sub", "grp", None), P(("sub", "grp")))
    out_specs = P("sub", None, None, None)
    return jax.shard_map(shards, mesh=mesh, in_specs=in_specs, out_specs=out_specs, check_vma=False)
```

```python
import jax
import jax.numpy as jnp
from jax import lax
from jax.experimental import pallas as pl
from jax.experimental.pallas import tpu as pltpu
from jax.sharding import PartitionSpec as P


def from_behind(x, axis, by):
    length = lax.axis_size(axis)
    pairs = [(i, i + by) for i in range(length) if 0 <= i + by < length]
    return lax.ppermute(x, axis, pairs)


def gram_of(left_side, right_side):
    count = left_side.shape[0]
    return jnp.dot(
        left_side.reshape(count, -1),
        right_side.reshape(count, -1).T,
        preferred_element_type=jnp.float32,
    )


def weighted(weight, values):
    return (weight.astype(jnp.float32) * values.astype(jnp.float32)).astype(jnp.bfloat16)


def local_kernel(depth_ref, defl_ref, coeff_ref, out_ref):
    count, comps, rows, cols, depth = defl_ref.shape
    width = cols * depth
    lane = lax.broadcasted_iota(jnp.int32, (count, cols, depth), 2)
    live_mask = (lane < depth_ref[0]).astype(jnp.bfloat16)
    wide_lane = lax.broadcasted_iota(jnp.int32, (count, width), 1)
    last_z = (wide_lane & (depth - 1)) == depth - 1
    zero_slab = jnp.zeros((count, depth), jnp.float32)

    def flat(row, comp):
        tiles = (defl_ref[:, comp, row] * live_mask).astype(jnp.float32)
        turned = pltpu.einshape("kyz->ykz", tiles)
        return jnp.concatenate([turned[col] for col in range(cols)], axis=1).astype(jnp.bfloat16)

    def weight(entry, row):
        w = coeff_ref[entry, row]
        return jnp.concatenate([w[col:col + 1] for col in range(cols)], axis=1)

    def body(row, acc):
        has_next = row < rows - 1
        following_row = jnp.minimum(row + 1, rows - 1)
        w = [weight(e, row) for e in range(4)]
        lefts, rights = [], []
        for comp in range(comps):
            live = flat(row, comp)
            next_x = jnp.where(has_next, flat(following_row, comp), 0)
            next_y = jnp.concatenate([live[:, depth:], jnp.zeros_like(live[:, :depth])], axis=1)
            next_z = jnp.where(last_z, 0, pltpu.roll(live, width - 1, 1))
            step_x = live - next_x
            step_y = live - next_y
            step_z = live - next_z
            lefts += [live, step_x, step_y, step_z]
            rights += [w[0] * live, w[1] * step_x, w[2] * step_y, w[3] * step_z]
        left = jnp.concatenate(lefts, axis=1)
        right = jnp.concatenate(rights, axis=1)
        return acc + lax.dot_general(
            left, right, (((1,), (1,)), ((), ())), preferred_element_type=jnp.float32
        )

    out_ref[...] = lax.fori_loop(0, rows, body, jnp.zeros((count, count), jnp.float32))


def local_terms(deflation, coefficients, depths):
    count = deflation.shape[0]
    return pl.pallas_call(
        local_kernel,
        out_shape=jax.ShapeDtypeStruct((count, count), jnp.float32),
        in_specs=[pl.BlockSpec(memory_space=pltpu.SMEM)] + [pl.BlockSpec(memory_space=pltpu.VMEM)] * 2,
        out_specs=pl.BlockSpec(memory_space=pltpu.VMEM),
        cost_estimate=pl.CostEstimate(
            flops=2 * 4 * count * deflation.size,
            bytes_accessed=deflation.size * 2 + coefficients.size * 2,
            transcendentals=0,
        ),
    )(depths, deflation, coefficients)


def shards(deflation, stiffness, depths):
    cell_count = deflation.shape[2] * deflation.shape[3] * deflation.shape[4]
    normalizer = 1.0 / (24.0 * cell_count)
    live_mask = (lax.iota(jnp.int32, deflation.shape[4]) < depths[0]).astype(jnp.bfloat16)
    bottom_x = deflation[:, :, 0] * live_mask
    bottom_y = deflation[:, :, :, 0] * live_mask
    weight_top_x = stiffness[1, -1]
    weight_top_y = stiffness[2, :, -1]
    next_x = from_behind(bottom_x, "sub", -1)
    weight_low_x = from_behind(weight_top_x, "sub", 1)
    next_y = from_behind(bottom_y, "grp", -1)
    weight_low_y = from_behind(weight_top_y, "grp", 1)
    diagonal_block = local_terms(deflation, stiffness, depths)
    top_x = deflation[:, :, -1] * live_mask
    top_y = deflation[:, :, :, -1] * live_mask
    coupling_x = -gram_of(weighted(weight_top_x, top_x), next_x)
    coupling_y = -gram_of(weighted(weight_top_y, top_y), next_y)
    diagonal_block = diagonal_block + gram_of(bottom_x, weighted(weight_low_x, bottom_x))
    diagonal_block = diagonal_block + gram_of(bottom_y, weighted(weight_low_y, bottom_y))
    row_block = normalizer * jnp.concatenate([diagonal_block, coupling_x, coupling_y], axis=1)
    groups = lax.axis_size("grp")
    copies = jnp.broadcast_to(row_block[None, None], (1, groups) + row_block.shape)
    return lax.all_to_all(copies, "grp", 1, 1, tiled=True)


def solution(mesh):
    in_specs = (P(None, None, "sub", "grp", None), P(None, "sub", "grp", None), P(("sub", "grp")))
    out_specs = P("sub", None, None, None)
    return jax.shard_map(shards, mesh=mesh, in_specs=in_specs, out_specs=out_specs, check_vma=False)
```

```python
import jax
import jax.numpy as jnp
from jax import lax
from jax.experimental import pallas as pl
from jax.experimental.pallas import tpu as pltpu
from jax.sharding import PartitionSpec as P


def from_behind(x, axis, by):
    length = lax.axis_size(axis)
    pairs = [(i, i + by) for i in range(length) if 0 <= i + by < length]
    return lax.ppermute(x, axis, pairs)


def gram_of(left_side, right_side):
    count = left_side.shape[0]
    return jnp.dot(
        left_side.reshape(count, -1),
        right_side.reshape(count, -1).T,
        preferred_element_type=jnp.float32,
    )


def weighted(weight, values):
    return (weight.astype(jnp.float32) * values.astype(jnp.float32)).astype(jnp.bfloat16)


def turn_kernel(depth_ref, defl_ref, live_ref, edge_ref):
    count, comps, rows, cols, depth = defl_ref.shape
    lane = lax.broadcasted_iota(jnp.int32, (count, cols, depth), 2)
    live_mask = (lane < depth_ref[0]).astype(jnp.bfloat16)

    def body(row, carry):
        for comp in range(comps):
            tiles = (defl_ref[:, comp, row] * live_mask).astype(jnp.float32)
            turned = pltpu.einshape("kyz->ykz", tiles).astype(jnp.bfloat16)
            for col in range(cols):
                live_ref[comp, row, :, pl.ds(col * depth, depth)] = turned[col]
            edge_ref[0, comp, row] = turned[0]
            edge_ref[1, comp, row] = turned[cols - 1]
        return carry

    lax.fori_loop(0, rows, body, 0)


def local_kernel(live_ref, coeff_ref, out_ref):
    comps, rows, count, width = live_ref.shape
    cols, depth = coeff_ref.shape[2:]
    lane = lax.broadcasted_iota(jnp.int32, (count, width), 1)
    last_z = (lane & (depth - 1)) == depth - 1

    def weight(entry, row):
        w = coeff_ref[entry, row]
        return jnp.concatenate([w[col:col + 1] for col in range(cols)], axis=1)

    def body(row, acc):
        has_next = row < rows - 1
        following_row = jnp.minimum(row + 1, rows - 1)
        w = [weight(e, row) for e in range(4)]
        lefts, rights = [], []
        for comp in range(comps):
            live = live_ref[comp, row]
            next_x = jnp.where(has_next, live_ref[comp, following_row], 0)
            next_y = jnp.concatenate([live[:, depth:], jnp.zeros_like(live[:, :depth])], axis=1)
            next_z = jnp.where(last_z, 0, pltpu.roll(live, width - 1, 1))
            step_x = live - next_x
            step_y = live - next_y
            step_z = live - next_z
            lefts += [live, step_x, step_y, step_z]
            rights += [w[0] * live, w[1] * step_x, w[2] * step_y, w[3] * step_z]
        left = jnp.concatenate(lefts, axis=1)
        right = jnp.concatenate(rights, axis=1)
        return acc + lax.dot_general(
            left, right, (((1,), (1,)), ((), ())), preferred_element_type=jnp.float32
        )

    out_ref[...] = lax.fori_loop(0, rows, body, jnp.zeros((count, count), jnp.float32))


def turned_field(deflation, depths):
    count, comps, rows, cols, depth = deflation.shape
    return pl.pallas_call(
        turn_kernel,
        out_shape=(
            jax.ShapeDtypeStruct((comps, rows, count, cols * depth), jnp.bfloat16),
            jax.ShapeDtypeStruct((2, comps, rows, count, depth), jnp.bfloat16),
        ),
        in_specs=[pl.BlockSpec(memory_space=pltpu.SMEM), pl.BlockSpec(memory_space=pltpu.VMEM)],
        out_specs=(pl.BlockSpec(memory_space=pltpu.VMEM), pl.BlockSpec(memory_space=pltpu.VMEM)),
        cost_estimate=pl.CostEstimate(flops=0, bytes_accessed=deflation.size * 5, transcendentals=0),
    )(depths, deflation)


def local_terms(live_t, coefficients):
    count = live_t.shape[2]
    return pl.pallas_call(
        local_kernel,
        out_shape=jax.ShapeDtypeStruct((count, count), jnp.float32),
        in_specs=[pl.BlockSpec(memory_space=pltpu.VMEM)] * 2,
        out_specs=pl.BlockSpec(memory_space=pltpu.VMEM),
        cost_estimate=pl.CostEstimate(
            flops=2 * 4 * count * live_t.size,
            bytes_accessed=live_t.size * 2 + coefficients.size * 2,
            transcendentals=0,
        ),
    )(live_t, coefficients)


def face_gram(left_side, right_side):
    return jnp.einsum("cxkz,cxlz->kl", left_side, right_side, preferred_element_type=jnp.float32)


def shards(deflation, stiffness, depths):
    cell_count = deflation.shape[2] * deflation.shape[3] * deflation.shape[4]
    normalizer = 1.0 / (24.0 * cell_count)
    live_mask = (lax.iota(jnp.int32, deflation.shape[4]) < depths[0]).astype(jnp.bfloat16)
    bottom_x = deflation[:, :, 0] * live_mask
    weight_top_x = stiffness[1, -1]
    weight_top_y = stiffness[2, :, -1]
    next_x = from_behind(bottom_x, "sub", -1)
    weight_low_x = from_behind(weight_top_x, "sub", 1)
    weight_low_y = from_behind(weight_top_y, "grp", 1)
    live_t, edges = turned_field(deflation, depths)
    bottom_y, top_y = edges[0], edges[1]
    next_y = from_behind(bottom_y, "grp", -1)
    diagonal_block = local_terms(live_t, stiffness)
    top_x = deflation[:, :, -1] * live_mask
    coupling_x = -gram_of(weighted(weight_top_x, top_x), next_x)
    coupling_y = -face_gram(weighted(weight_top_y[None, :, None], top_y), next_y)
    diagonal_block = diagonal_block + gram_of(bottom_x, weighted(weight_low_x, bottom_x))
    diagonal_block = diagonal_block + face_gram(bottom_y, weighted(weight_low_y[None, :, None], bottom_y))
    row_block = normalizer * jnp.concatenate([diagonal_block, coupling_x, coupling_y], axis=1)
    groups = lax.axis_size("grp")
    copies = jnp.broadcast_to(row_block[None, None], (1, groups) + row_block.shape)
    return lax.all_to_all(copies, "grp", 1, 1, tiled=True)


def solution(mesh):
    in_specs = (P(None, None, "sub", "grp", None), P(None, "sub", "grp", None), P(("sub", "grp")))
    out_specs = P("sub", None, None, None)
    return jax.shard_map(shards, mesh=mesh, in_specs=in_specs, out_specs=out_specs, check_vma=False)
```

```python
import jax
import jax.numpy as jnp
from jax import lax
from jax.experimental import pallas as pl
from jax.experimental.pallas import tpu as pltpu
from jax.sharding import PartitionSpec as P


def from_behind(x, axis, by):
    length = lax.axis_size(axis)
    pairs = [(i, i + by) for i in range(length) if 0 <= i + by < length]
    return lax.ppermute(x, axis, pairs)


def gram_of(left_side, right_side):
    count = left_side.shape[0]
    return jnp.dot(
        left_side.reshape(count, -1),
        right_side.reshape(count, -1).T,
        preferred_element_type=jnp.float32,
    )


def weighted(weight, values):
    return (weight.astype(jnp.float32) * values.astype(jnp.float32)).astype(jnp.bfloat16)


def turn_kernel(depth_ref, defl_ref, live_ref, edge_ref):
    count, comps, rows, cols, depth = defl_ref.shape
    lane = lax.broadcasted_iota(jnp.int32, (count, cols, depth), 2)
    live_mask = (lane < depth_ref[0]).astype(jnp.bfloat16)

    def body(row, carry):
        for comp in range(comps):
            tiles = (defl_ref[:, comp, row] * live_mask).astype(jnp.float32)
            turned = pltpu.einshape("kyz->ykz", tiles).astype(jnp.bfloat16)
            for col in range(cols):
                live_ref[comp, row, :, pl.ds(col * depth, depth)] = turned[col]
            edge_ref[0, comp, row] = turned[0]
            edge_ref[1, comp, row] = turned[cols - 1]
        return carry

    lax.fori_loop(0, rows, body, 0, unroll=4)


def local_kernel(live_ref, coeff_ref, out_ref):
    comps, rows, count, width = live_ref.shape
    cols, depth = coeff_ref.shape[2:]
    lane = lax.broadcasted_iota(jnp.int32, (count, width), 1)
    last_z = (lane & (depth - 1)) == depth - 1

    def weight(entry, row):
        w = coeff_ref[entry, row]
        return jnp.concatenate([w[col:col + 1] for col in range(cols)], axis=1)

    def body(row, acc):
        has_next = row < rows - 1
        following_row = jnp.minimum(row + 1, rows - 1)
        w = [weight(e, row) for e in range(4)]
        lefts, rights = [], []
        for comp in range(comps):
            live = live_ref[comp, row]
            next_x = jnp.where(has_next, live_ref[comp, following_row], 0)
            next_y = jnp.concatenate([live[:, depth:], jnp.zeros_like(live[:, :depth])], axis=1)
            next_z = jnp.where(last_z, 0, pltpu.roll(live, width - 1, 1))
            step_x = live - next_x
            step_y = live - next_y
            step_z = live - next_z
            lefts += [live, step_x, step_y, step_z]
            rights += [w[0] * live, w[1] * step_x, w[2] * step_y, w[3] * step_z]
        left = jnp.concatenate(lefts, axis=1)
        right = jnp.concatenate(rights, axis=1)
        return acc + lax.dot_general(
            left, right, (((1,), (1,)), ((), ())), preferred_element_type=jnp.float32
        )

    out_ref[...] = lax.fori_loop(0, rows, body, jnp.zeros((count, count), jnp.float32), unroll=8)


def turned_field(deflation, depths):
    count, comps, rows, cols, depth = deflation.shape
    return pl.pallas_call(
        turn_kernel,
        out_shape=(
            jax.ShapeDtypeStruct((comps, rows, count, cols * depth), jnp.bfloat16),
            jax.ShapeDtypeStruct((2, comps, rows, count, depth), jnp.bfloat16),
        ),
        in_specs=[pl.BlockSpec(memory_space=pltpu.SMEM), pl.BlockSpec(memory_space=pltpu.VMEM)],
        out_specs=(pl.BlockSpec(memory_space=pltpu.VMEM), pl.BlockSpec(memory_space=pltpu.VMEM)),
        cost_estimate=pl.CostEstimate(flops=0, bytes_accessed=deflation.size * 5, transcendentals=0),
    )(depths, deflation)


def local_terms(live_t, coefficients):
    count = live_t.shape[2]
    return pl.pallas_call(
        local_kernel,
        out_shape=jax.ShapeDtypeStruct((count, count), jnp.float32),
        in_specs=[pl.BlockSpec(memory_space=pltpu.VMEM)] * 2,
        out_specs=pl.BlockSpec(memory_space=pltpu.VMEM),
        cost_estimate=pl.CostEstimate(
            flops=2 * 4 * count * live_t.size,
            bytes_accessed=live_t.size * 2 + coefficients.size * 2,
            transcendentals=0,
        ),
    )(live_t, coefficients)


def face_gram(left_side, right_side):
    return jnp.einsum("cxkz,cxlz->kl", left_side, right_side, preferred_element_type=jnp.float32)


def shards(deflation, stiffness, depths):
    cell_count = deflation.shape[2] * deflation.shape[3] * deflation.shape[4]
    normalizer = 1.0 / (24.0 * cell_count)
    live_mask = (lax.iota(jnp.int32, deflation.shape[4]) < depths[0]).astype(jnp.bfloat16)
    bottom_x = deflation[:, :, 0] * live_mask
    weight_top_x = stiffness[1, -1]
    weight_top_y = stiffness[2, :, -1]
    next_x = from_behind(bottom_x, "sub", -1)
    weight_low_x = from_behind(weight_top_x, "sub", 1)
    weight_low_y = from_behind(weight_top_y, "grp", 1)
    live_t, edges = turned_field(deflation, depths)
    bottom_y, top_y = edges[0], edges[1]
    next_y = from_behind(bottom_y, "grp", -1)
    diagonal_block = local_terms(live_t, stiffness)
    top_x = deflation[:, :, -1] * live_mask
    coupling_x = -gram_of(weighted(weight_top_x, top_x), next_x)
    coupling_y = -face_gram(weighted(weight_top_y[None, :, None], top_y), next_y)
    diagonal_block = diagonal_block + gram_of(bottom_x, weighted(weight_low_x, bottom_x))
    diagonal_block = diagonal_block + face_gram(bottom_y, weighted(weight_low_y[None, :, None], bottom_y))
    row_block = normalizer * jnp.concatenate([diagonal_block, coupling_x, coupling_y], axis=1)
    groups = lax.axis_size("grp")
    copies = jnp.broadcast_to(row_block[None, None], (1, groups) + row_block.shape)
    return lax.all_to_all(copies, "grp", 1, 1, tiled=True)


def solution(mesh):
    in_specs = (P(None, None, "sub", "grp", None), P(None, "sub", "grp", None), P(("sub", "grp")))
    out_specs = P("sub", None, None, None)
    return jax.shard_map(shards, mesh=mesh, in_specs=in_specs, out_specs=out_specs, check_vma=False)
```

```python
import jax
import jax.numpy as jnp
from jax import lax
from jax.experimental import pallas as pl
from jax.experimental.pallas import tpu as pltpu
from jax.sharding import PartitionSpec as P


def from_behind(x, axis, by):
    length = lax.axis_size(axis)
    pairs = [(i, i + by) for i in range(length) if 0 <= i + by < length]
    return lax.ppermute(x, axis, pairs)


def gram_of(left_side, right_side):
    count = left_side.shape[0]
    return jnp.dot(
        left_side.reshape(count, -1),
        right_side.reshape(count, -1).T,
        preferred_element_type=jnp.float32,
    )


def weighted(weight, values):
    return (weight.astype(jnp.float32) * values.astype(jnp.float32)).astype(jnp.bfloat16)


def turn_kernel(depth_ref, defl_ref, live_ref, low_ref, high_ref, first_ref):
    count, comps, rows, cols, depth = defl_ref.shape
    lane = lax.broadcasted_iota(jnp.int32, (count, cols, depth), 2)
    live_mask = (lane < depth_ref[0]).astype(jnp.bfloat16)

    def body(row, carry):
        for comp in range(comps):
            tiles = (defl_ref[:, comp, row] * live_mask).astype(jnp.float32)
            turned = pltpu.einshape("kyz->ykz", tiles).astype(jnp.bfloat16)
            for col in range(cols):
                live_ref[comp, row, :, pl.ds(col * depth, depth)] = turned[col]
            low_ref[comp, row] = turned[0]
            high_ref[comp, row] = turned[cols - 1]

            @pl.when(row == 0)
            def _():
                for col in range(cols):
                    first_ref[comp, :, pl.ds(col * depth, depth)] = turned[col]

        return carry

    lax.fori_loop(0, rows, body, 0, unroll=4)


def local_kernel(live_ref, coeff_ref, out_ref):
    comps, rows, count, width = live_ref.shape
    cols, depth = coeff_ref.shape[2:]
    lane = lax.broadcasted_iota(jnp.int32, (count, width), 1)
    last_z = (lane & (depth - 1)) == depth - 1

    def weight(entry, row):
        w = coeff_ref[entry, row]
        return jnp.concatenate([w[col:col + 1] for col in range(cols)], axis=1)

    def body(row, acc):
        has_next = row < rows - 1
        following_row = jnp.minimum(row + 1, rows - 1)
        w = [weight(e, row) for e in range(4)]
        lefts, rights = [], []
        for comp in range(comps):
            live = live_ref[comp, row]
            next_x = jnp.where(has_next, live_ref[comp, following_row], 0)
            next_y = jnp.concatenate([live[:, depth:], jnp.zeros_like(live[:, :depth])], axis=1)
            next_z = jnp.where(last_z, 0, pltpu.roll(live, width - 1, 1))
            step_x = live - next_x
            step_y = live - next_y
            step_z = live - next_z
            lefts += [live, step_x, step_y, step_z]
            rights += [w[0] * live, w[1] * step_x, w[2] * step_y, w[3] * step_z]
        left = jnp.concatenate(lefts, axis=1)
        right = jnp.concatenate(rights, axis=1)
        return acc + lax.dot_general(
            left, right, (((1,), (1,)), ((), ())), preferred_element_type=jnp.float32
        )

    out_ref[...] = lax.fori_loop(0, rows, body, jnp.zeros((count, count), jnp.float32), unroll=8)


def turned_field(deflation, depths):
    count, comps, rows, cols, depth = deflation.shape
    return pl.pallas_call(
        turn_kernel,
        out_shape=(
            jax.ShapeDtypeStruct((comps, rows, count, cols * depth), jnp.bfloat16),
            jax.ShapeDtypeStruct((comps, rows, count, depth), jnp.bfloat16),
            jax.ShapeDtypeStruct((comps, rows, count, depth), jnp.bfloat16),
            jax.ShapeDtypeStruct((comps, count, cols * depth), jnp.bfloat16),
        ),
        in_specs=[pl.BlockSpec(memory_space=pltpu.SMEM), pl.BlockSpec(memory_space=pltpu.VMEM)],
        out_specs=(pl.BlockSpec(memory_space=pltpu.VMEM),) * 4,
        cost_estimate=pl.CostEstimate(flops=0, bytes_accessed=deflation.size * 5, transcendentals=0),
    )(depths, deflation)


def local_terms(live_t, coefficients):
    count = live_t.shape[2]
    return pl.pallas_call(
        local_kernel,
        out_shape=jax.ShapeDtypeStruct((count, count), jnp.float32),
        in_specs=[pl.BlockSpec(memory_space=pltpu.VMEM)] * 2,
        out_specs=pl.BlockSpec(memory_space=pltpu.VMEM),
        cost_estimate=pl.CostEstimate(
            flops=2 * 4 * count * live_t.size,
            bytes_accessed=live_t.size * 2 + coefficients.size * 2,
            transcendentals=0,
        ),
    )(live_t, coefficients)


def face_gram(left_side, right_side):
    return jnp.einsum("cxkz,cxlz->kl", left_side, right_side, preferred_element_type=jnp.float32)


def layer_gram(left_side, right_side):
    return jnp.einsum("ckj,clj->kl", left_side, right_side, preferred_element_type=jnp.float32)


def shards(deflation, stiffness, depths):
    cell_count = deflation.shape[2] * deflation.shape[3] * deflation.shape[4]
    normalizer = 1.0 / (24.0 * cell_count)
    live_t, bottom_y, top_y, bottom_x = turned_field(deflation, depths)
    weight_top_x = stiffness[1, -1].reshape(-1)
    weight_top_y = stiffness[2, :, -1]
    live_t, bottom_y, bottom_x, weight_top_x, weight_top_y = lax.optimization_barrier(
        (live_t, bottom_y, bottom_x, weight_top_x, weight_top_y)
    )
    next_y = from_behind(bottom_y, "grp", -1)
    next_x = from_behind(bottom_x, "sub", -1)
    weight_low_x = from_behind(weight_top_x, "sub", 1)
    weight_low_y = from_behind(weight_top_y, "grp", 1)
    diagonal_block = local_terms(live_t, stiffness)
    top_x = live_t[:, -1]
    coupling_x = -layer_gram(weighted(weight_top_x, top_x), next_x)
    coupling_y = -face_gram(weighted(weight_top_y[None, :, None], top_y), next_y)
    diagonal_block = diagonal_block + layer_gram(bottom_x, weighted(weight_low_x, bottom_x))
    diagonal_block = diagonal_block + face_gram(bottom_y, weighted(weight_low_y[None, :, None], bottom_y))
    row_block = normalizer * jnp.concatenate([diagonal_block, coupling_x, coupling_y], axis=1)
    groups = lax.axis_size("grp")
    copies = jnp.broadcast_to(row_block[None, None], (1, groups) + row_block.shape)
    return lax.all_to_all(copies, "grp", 1, 1, tiled=True)


def solution(mesh):
    in_specs = (P(None, None, "sub", "grp", None), P(None, "sub", "grp", None), P(("sub", "grp")))
    out_specs = P("sub", None, None, None)
    return jax.shard_map(shards, mesh=mesh, in_specs=in_specs, out_specs=out_specs, check_vma=False)
```

```python
import jax
import jax.numpy as jnp
from jax import lax
from jax.experimental import pallas as pl
from jax.experimental.pallas import tpu as pltpu
from jax.sharding import PartitionSpec as P


def from_behind(x, axis, by):
    length = lax.axis_size(axis)
    pairs = [(i, i + by) for i in range(length) if 0 <= i + by < length]
    return lax.ppermute(x, axis, pairs)


def gram_of(left_side, right_side):
    count = left_side.shape[0]
    return jnp.dot(
        left_side.reshape(count, -1),
        right_side.reshape(count, -1).T,
        preferred_element_type=jnp.float32,
    )


def weighted(weight, values):
    return (weight.astype(jnp.float32) * values.astype(jnp.float32)).astype(jnp.bfloat16)


def turn_kernel(depth_ref, defl_ref, live_ref, low_ref, high_ref, first_ref):
    count, comps, rows, cols, depth = defl_ref.shape
    lane = lax.broadcasted_iota(jnp.int32, (count, cols, depth), 2)
    live_mask = (lane < depth_ref[0]).astype(jnp.bfloat16)

    def body(row, carry):
        for comp in range(comps):
            tiles = (defl_ref[:, comp, row] * live_mask).astype(jnp.float32)
            turned = pltpu.einshape("kyz->ykz", tiles).astype(jnp.bfloat16)
            for col in range(cols):
                live_ref[comp, row, :, pl.ds(col * depth, depth)] = turned[col]
            low_ref[comp, row] = turned[0]
            high_ref[comp, row] = turned[cols - 1]

            @pl.when(row == 0)
            def _():
                for col in range(cols):
                    first_ref[comp, :, pl.ds(col * depth, depth)] = turned[col]

        return carry

    lax.fori_loop(0, rows, body, 0, unroll=4)


def local_kernel(live_ref, coeff_ref, out_ref):
    comps, rows, count, width = live_ref.shape
    cols, depth = coeff_ref.shape[2:]
    lane = lax.broadcasted_iota(jnp.int32, (count, width), 1)
    last_z = (lane & (depth - 1)) == depth - 1

    def weight(entry, row):
        w = coeff_ref[entry, row]
        return jnp.concatenate([w[col:col + 1] for col in range(cols)], axis=1)

    def body(row, acc):
        has_next = row < rows - 1
        following_row = jnp.minimum(row + 1, rows - 1)
        w = [weight(e, row) for e in range(4)]
        lefts, rights = [], []
        for comp in range(comps):
            live = live_ref[comp, row]
            next_x = jnp.where(has_next, live_ref[comp, following_row], 0)
            next_y = jnp.concatenate([live[:, depth:], jnp.zeros_like(live[:, :depth])], axis=1)
            next_z = jnp.where(last_z, 0, pltpu.roll(live, width - 1, 1))
            step_x = live - next_x
            step_y = live - next_y
            step_z = live - next_z
            lefts += [live, step_x, step_y, step_z]
            rights += [w[0] * live, w[1] * step_x, w[2] * step_y, w[3] * step_z]
        left = jnp.concatenate(lefts, axis=1)
        right = jnp.concatenate(rights, axis=1)
        return acc + lax.dot_general(
            left, right, (((1,), (1,)), ((), ())), preferred_element_type=jnp.float32
        )

    out_ref[...] = lax.fori_loop(0, rows, body, jnp.zeros((count, count), jnp.float32), unroll=8)


def turned_field(deflation, depths):
    count, comps, rows, cols, depth = deflation.shape
    return pl.pallas_call(
        turn_kernel,
        out_shape=(
            jax.ShapeDtypeStruct((comps, rows, count, cols * depth), jnp.bfloat16),
            jax.ShapeDtypeStruct((comps, rows, count, depth), jnp.bfloat16),
            jax.ShapeDtypeStruct((comps, rows, count, depth), jnp.bfloat16),
            jax.ShapeDtypeStruct((comps, count, cols * depth), jnp.bfloat16),
        ),
        in_specs=[pl.BlockSpec(memory_space=pltpu.SMEM), pl.BlockSpec(memory_space=pltpu.VMEM)],
        out_specs=(pl.BlockSpec(memory_space=pltpu.VMEM),) * 4,
        cost_estimate=pl.CostEstimate(flops=0, bytes_accessed=deflation.size * 5, transcendentals=0),
    )(depths, deflation)


def local_terms(live_t, coefficients):
    count = live_t.shape[2]
    return pl.pallas_call(
        local_kernel,
        out_shape=jax.ShapeDtypeStruct((count, count), jnp.float32),
        in_specs=[pl.BlockSpec(memory_space=pltpu.VMEM)] * 2,
        out_specs=pl.BlockSpec(memory_space=pltpu.VMEM),
        cost_estimate=pl.CostEstimate(
            flops=2 * 4 * count * live_t.size,
            bytes_accessed=live_t.size * 2 + coefficients.size * 2,
            transcendentals=0,
        ),
    )(live_t, coefficients)


def face_gram(left_side, right_side):
    return jnp.einsum("cxkz,cxlz->kl", left_side, right_side, preferred_element_type=jnp.float32)


def layer_gram(left_side, right_side):
    return jnp.einsum("ckj,clj->kl", left_side, right_side, preferred_element_type=jnp.float32)


def shards(deflation, stiffness, depths):
    cell_count = deflation.shape[2] * deflation.shape[3] * deflation.shape[4]
    normalizer = 1.0 / (24.0 * cell_count)
    live_t, bottom_y, top_y, bottom_x = turned_field(deflation, depths)
    weight_top_x = stiffness[1, -1].reshape(-1)
    weight_top_y = stiffness[2, :, -1]
    live_t, bottom_y, bottom_x = lax.optimization_barrier((live_t, bottom_y, bottom_x))
    next_y = from_behind(bottom_y, "grp", -1)
    next_x = from_behind(bottom_x, "sub", -1)
    weight_low_x = from_behind(weight_top_x, "sub", 1)
    weight_low_y = from_behind(weight_top_y, "grp", 1)
    diagonal_block = local_terms(live_t, stiffness)
    top_x = live_t[:, -1]
    coupling_x = -layer_gram(weighted(weight_top_x, top_x), next_x)
    diagonal_block = diagonal_block + layer_gram(bottom_x, weighted(weight_low_x, bottom_x))
    diagonal_block = diagonal_block + face_gram(bottom_y, weighted(weight_low_y[None, :, None], bottom_y))
    coupling_y = -face_gram(weighted(weight_top_y[None, :, None], top_y), next_y)
    row_block = normalizer * jnp.concatenate([diagonal_block, coupling_x, coupling_y], axis=1)
    groups = lax.axis_size("grp")
    copies = jnp.broadcast_to(row_block[None, None], (1, groups) + row_block.shape)
    return lax.all_to_all(copies, "grp", 1, 1, tiled=True)


def solution(mesh):
    in_specs = (P(None, None, "sub", "grp", None), P(None, "sub", "grp", None), P(("sub", "grp")))
    out_specs = P("sub", None, None, None)
    return jax.shard_map(shards, mesh=mesh, in_specs=in_specs, out_specs=out_specs, check_vma=False)
```

```python
import jax
import jax.numpy as jnp
from jax import lax
from jax.experimental import pallas as pl
from jax.experimental.pallas import tpu as pltpu
from jax.sharding import PartitionSpec as P


def from_behind(x, axis, by):
    length = lax.axis_size(axis)
    pairs = [(i, i + by) for i in range(length) if 0 <= i + by < length]
    return lax.ppermute(x, axis, pairs)


def gram_of(left_side, right_side):
    count = left_side.shape[0]
    return jnp.dot(
        left_side.reshape(count, -1),
        right_side.reshape(count, -1).T,
        preferred_element_type=jnp.float32,
    )


def weighted(weight, values):
    return (weight.astype(jnp.float32) * values.astype(jnp.float32)).astype(jnp.bfloat16)


def turn_kernel(depth_ref, defl_ref, live_ref, low_ref, high_ref, first_ref):
    count, comps, rows, cols, depth = defl_ref.shape
    lane = lax.broadcasted_iota(jnp.int32, (count, cols, depth), 2)
    live_mask = (lane < depth_ref[0]).astype(jnp.bfloat16)

    def body(row, carry):
        for comp in range(comps):
            tiles = (defl_ref[:, comp, row] * live_mask).astype(jnp.float32)
            turned = pltpu.einshape("kyz->ykz", tiles).astype(jnp.bfloat16)
            for col in range(cols):
                live_ref[comp, row, :, pl.ds(col * depth, depth)] = turned[col]
            low_ref[comp, row] = turned[0]
            high_ref[comp, row] = turned[cols - 1]

            @pl.when(row == 0)
            def _():
                for col in range(cols):
                    first_ref[comp, :, pl.ds(col * depth, depth)] = turned[col]

        return carry

    lax.fori_loop(0, rows, body, 0, unroll=4)


def local_kernel(live_ref, coeff_ref, out_ref):
    comps, rows, count, width = live_ref.shape
    cols, depth = coeff_ref.shape[2:]
    lane = lax.broadcasted_iota(jnp.int32, (count, width), 1)
    last_z = (lane & (depth - 1)) == depth - 1

    def weight(entry, row):
        w = coeff_ref[entry, row]
        return jnp.concatenate([w[col:col + 1] for col in range(cols)], axis=1)

    def body(row, acc):
        has_next = row < rows - 1
        following_row = jnp.minimum(row + 1, rows - 1)
        w = [weight(e, row) for e in range(4)]
        lefts, rights = [], []
        for comp in range(comps):
            live = live_ref[comp, row]
            next_x = jnp.where(has_next, live_ref[comp, following_row], 0)
            next_y = jnp.concatenate([live[:, depth:], jnp.zeros_like(live[:, :depth])], axis=1)
            next_z = jnp.where(last_z, 0, pltpu.roll(live, width - 1, 1))
            step_x = live - next_x
            step_y = live - next_y
            step_z = live - next_z
            lefts += [live, step_x, step_y, step_z]
            rights += [w[0] * live, w[1] * step_x, w[2] * step_y, w[3] * step_z]
        left = jnp.concatenate(lefts, axis=1)
        right = jnp.concatenate(rights, axis=1)
        return acc + lax.dot_general(
            left, right, (((1,), (1,)), ((), ())), preferred_element_type=jnp.float32
        )

    out_ref[...] = lax.fori_loop(0, rows, body, jnp.zeros((count, count), jnp.float32), unroll=8)


def turned_field(deflation, depths):
    count, comps, rows, cols, depth = deflation.shape
    return pl.pallas_call(
        turn_kernel,
        out_shape=(
            jax.ShapeDtypeStruct((comps, rows, count, cols * depth), jnp.bfloat16),
            jax.ShapeDtypeStruct((comps, rows, count, depth), jnp.bfloat16),
            jax.ShapeDtypeStruct((comps, rows, count, depth), jnp.bfloat16),
            jax.ShapeDtypeStruct((comps, count, cols * depth), jnp.bfloat16),
        ),
        in_specs=[pl.BlockSpec(memory_space=pltpu.SMEM), pl.BlockSpec(memory_space=pltpu.VMEM)],
        out_specs=(pl.BlockSpec(memory_space=pltpu.VMEM),) * 4,
        cost_estimate=pl.CostEstimate(flops=0, bytes_accessed=deflation.size * 5, transcendentals=0),
    )(depths, deflation)


def local_terms(live_t, coefficients):
    count = live_t.shape[2]
    return pl.pallas_call(
        local_kernel,
        out_shape=jax.ShapeDtypeStruct((count, count), jnp.float32),
        in_specs=[pl.BlockSpec(memory_space=pltpu.VMEM)] * 2,
        out_specs=pl.BlockSpec(memory_space=pltpu.VMEM),
        cost_estimate=pl.CostEstimate(
            flops=2 * 4 * count * live_t.size,
            bytes_accessed=live_t.size * 2 + coefficients.size * 2,
            transcendentals=0,
        ),
    )(live_t, coefficients)


def face_gram(left_side, right_side):
    return jnp.einsum("cxkz,cxlz->kl", left_side, right_side, preferred_element_type=jnp.float32)


def layer_gram(left_side, right_side):
    return jnp.einsum("ckj,clj->kl", left_side, right_side, preferred_element_type=jnp.float32)


def shards(deflation, stiffness, depths):
    cell_count = deflation.shape[2] * deflation.shape[3] * deflation.shape[4]
    normalizer = 1.0 / (24.0 * cell_count)
    live_t, bottom_y, top_y, bottom_x = turned_field(deflation, depths)
    weight_top_x = stiffness[1, -1].reshape(-1)
    weight_top_y = stiffness[2, :, -1]
    live_t, bottom_y, bottom_x, weight_top_x, weight_top_y = lax.optimization_barrier(
        (live_t, bottom_y, bottom_x, weight_top_x, weight_top_y)
    )
    next_y = from_behind(bottom_y, "grp", -1)
    next_x = from_behind(bottom_x, "sub", -1)
    weight_low_x = from_behind(weight_top_x, "sub", 1)
    weight_low_y = from_behind(weight_top_y, "grp", 1)
    diagonal_block = local_terms(live_t, stiffness)
    top_x = live_t[:, -1]
    coupling_x = -layer_gram(weighted(weight_top_x, top_x), next_x)
    coupling_y = -face_gram(weighted(weight_top_y[None, :, None], top_y), next_y)
    diagonal_block = diagonal_block + layer_gram(bottom_x, weighted(weight_low_x, bottom_x))
    diagonal_block = diagonal_block + face_gram(bottom_y, weighted(weight_low_y[None, :, None], bottom_y))
    row_block = normalizer * jnp.concatenate([diagonal_block, coupling_x, coupling_y], axis=1)
    groups = lax.axis_size("grp")
    dense = row_block.reshape(-1, 128)
    copies = jnp.broadcast_to(dense[None, None], (1, groups) + dense.shape)
    gathered = lax.all_to_all(copies, "grp", 1, 1, tiled=True)
    return gathered.reshape((1, groups) + row_block.shape)


def solution(mesh):
    in_specs = (P(None, None, "sub", "grp", None), P(None, "sub", "grp", None), P(("sub", "grp")))
    out_specs = P("sub", None, None, None)
    return jax.shard_map(shards, mesh=mesh, in_specs=in_specs, out_specs=out_specs, check_vma=False)
```

```python
import jax
import jax.numpy as jnp
from jax import lax
from jax.experimental import pallas as pl
from jax.experimental.pallas import tpu as pltpu
from jax.sharding import PartitionSpec as P


def from_behind(x, axis, by):
    length = lax.axis_size(axis)
    pairs = [(i, i + by) for i in range(length) if 0 <= i + by < length]
    return lax.ppermute(x, axis, pairs)


def gram_of(left_side, right_side):
    count = left_side.shape[0]
    return jnp.dot(
        left_side.reshape(count, -1),
        right_side.reshape(count, -1).T,
        preferred_element_type=jnp.float32,
    )


def weighted(weight, values):
    return (weight.astype(jnp.float32) * values.astype(jnp.float32)).astype(jnp.bfloat16)


def local_kernel(depth_ref, defl_ref, coeff_ref, out_ref):
    count, comps, rows, cols, depth = defl_ref.shape
    width = cols * depth
    lane = lax.broadcasted_iota(jnp.int32, (count, cols, depth), 2)
    live_mask = (lane < depth_ref[0]).astype(jnp.bfloat16)
    wide_lane = lax.broadcasted_iota(jnp.int32, (count, width), 1)
    last_z = (wide_lane & (depth - 1)) == depth - 1
    zero_slab = jnp.zeros((count, depth), jnp.float32)

    def flat(row, comp):
        tiles = (defl_ref[:, comp, row] * live_mask).astype(jnp.float32)
        turned = pltpu.einshape("kyz->ykz", tiles)
        return jnp.concatenate([turned[col] for col in range(cols)], axis=1).astype(jnp.bfloat16)

    def weight(entry, row):
        w = coeff_ref[entry, row]
        return jnp.concatenate([w[col:col + 1] for col in range(cols)], axis=1)

    def body(row, acc):
        has_next = row < rows - 1
        following_row = jnp.minimum(row + 1, rows - 1)
        w = [weight(e, row) for e in range(4)]
        lefts, rights = [], []
        for comp in range(comps):
            live = flat(row, comp)
            next_x = jnp.where(has_next, flat(following_row, comp), 0)
            next_y = jnp.concatenate([live[:, depth:], jnp.zeros_like(live[:, :depth])], axis=1)
            next_z = jnp.where(last_z, 0, pltpu.roll(live, width - 1, 1))
            step_x = live - next_x
            step_y = live - next_y
            step_z = live - next_z
            lefts += [live, step_x, step_y, step_z]
            rights += [w[0] * live, w[1] * step_x, w[2] * step_y, w[3] * step_z]
        left = jnp.concatenate(lefts, axis=1)
        right = jnp.concatenate(rights, axis=1)
        return acc + lax.dot_general(
            left, right, (((1,), (1,)), ((), ())), preferred_element_type=jnp.float32
        )

    out_ref[...] = lax.fori_loop(0, rows, body, jnp.zeros((count, count), jnp.float32), unroll=8)


def local_terms(deflation, coefficients, depths):
    count = deflation.shape[0]
    return pl.pallas_call(
        local_kernel,
        out_shape=jax.ShapeDtypeStruct((count, count), jnp.float32),
        in_specs=[pl.BlockSpec(memory_space=pltpu.SMEM)] + [pl.BlockSpec(memory_space=pltpu.VMEM)] * 2,
        out_specs=pl.BlockSpec(memory_space=pltpu.VMEM),
        cost_estimate=pl.CostEstimate(
            flops=2 * 4 * count * deflation.size,
            bytes_accessed=deflation.size * 2 + coefficients.size * 2,
            transcendentals=0,
        ),
    )(depths, deflation, coefficients)


def shards(deflation, stiffness, depths):
    cell_count = deflation.shape[2] * deflation.shape[3] * deflation.shape[4]
    normalizer = 1.0 / (24.0 * cell_count)
    live_mask = (lax.iota(jnp.int32, deflation.shape[4]) < depths[0]).astype(jnp.bfloat16)
    bottom_x = deflation[:, :, 0] * live_mask
    bottom_y = deflation[:, :, :, 0] * live_mask
    weight_top_x = stiffness[1, -1]
    weight_top_y = stiffness[2, :, -1]
    next_x = from_behind(bottom_x, "sub", -1)
    weight_low_x = from_behind(weight_top_x, "sub", 1)
    next_y = from_behind(bottom_y, "grp", -1)
    weight_low_y = from_behind(weight_top_y, "grp", 1)
    diagonal_block = local_terms(deflation, stiffness, depths)
    top_x = deflation[:, :, -1] * live_mask
    top_y = deflation[:, :, :, -1] * live_mask
    coupling_x = -gram_of(weighted(weight_top_x, top_x), next_x)
    coupling_y = -gram_of(weighted(weight_top_y, top_y), next_y)
    diagonal_block = diagonal_block + gram_of(bottom_x, weighted(weight_low_x, bottom_x))
    diagonal_block = diagonal_block + gram_of(bottom_y, weighted(weight_low_y, bottom_y))
    row_block = normalizer * jnp.concatenate([diagonal_block, coupling_x, coupling_y], axis=1)
    groups = lax.axis_size("grp")
    dense = row_block.reshape(-1, 128)
    copies = jnp.broadcast_to(dense[None, None], (1, groups) + dense.shape)
    gathered = lax.all_to_all(copies, "grp", 1, 1, tiled=True)
    return gathered.reshape((1, groups) + row_block.shape)


def solution(mesh):
    in_specs = (P(None, None, "sub", "grp", None), P(None, "sub", "grp", None), P(("sub", "grp")))
    out_specs = P("sub", None, None, None)
    return jax.shard_map(shards, mesh=mesh, in_specs=in_specs, out_specs=out_specs, check_vma=False)
```

```python
import jax
import jax.numpy as jnp
from jax import lax
from jax.experimental import pallas as pl
from jax.experimental.pallas import tpu as pltpu
from jax.sharding import PartitionSpec as P


def from_behind(x, axis, by):
    length = lax.axis_size(axis)
    pairs = [(i, i + by) for i in range(length) if 0 <= i + by < length]
    return lax.ppermute(x, axis, pairs)


def gram_of(left_side, right_side):
    count = left_side.shape[0]
    return jnp.dot(
        left_side.reshape(count, -1),
        right_side.reshape(count, -1).T,
        preferred_element_type=jnp.float32,
    )


def weighted(weight, values):
    return (weight.astype(jnp.float32) * values.astype(jnp.float32)).astype(jnp.bfloat16)


def low_kernel(depth_ref, defl_ref, low_ref):
    count, comps, rows, cols, depth = defl_ref.shape
    lane = lax.broadcasted_iota(jnp.int32, (count, depth), 1)
    live_mask = (lane < depth_ref[0]).astype(jnp.bfloat16)
    for comp in range(comps):

        def body(row, carry):
            low_ref[comp, row] = defl_ref[:, comp, row, 0, :] * live_mask
            return carry

        lax.fori_loop(0, rows, body, 0, unroll=4)


def low_layer(deflation, depths):
    count, comps, rows, cols, depth = deflation.shape
    return pl.pallas_call(
        low_kernel,
        out_shape=jax.ShapeDtypeStruct((comps, rows, count, depth), jnp.bfloat16),
        in_specs=[pl.BlockSpec(memory_space=pltpu.SMEM), pl.BlockSpec(memory_space=pltpu.VMEM)],
        out_specs=pl.BlockSpec(memory_space=pltpu.VMEM),
        cost_estimate=pl.CostEstimate(flops=0, bytes_accessed=deflation.size * 2, transcendentals=0),
    )(depths, deflation)


def turn_kernel(depth_ref, defl_ref, live_ref, low_ref, high_ref, first_ref):
    count, comps, rows, cols, depth = defl_ref.shape
    lane = lax.broadcasted_iota(jnp.int32, (count, cols, depth), 2)
    live_mask = (lane < depth_ref[0]).astype(jnp.bfloat16)

    def body(row, carry):
        for comp in range(comps):
            tiles = (defl_ref[:, comp, row] * live_mask).astype(jnp.float32)
            turned = pltpu.einshape("kyz->ykz", tiles).astype(jnp.bfloat16)
            for col in range(cols):
                live_ref[comp, row, :, pl.ds(col * depth, depth)] = turned[col]
            low_ref[comp, row] = turned[0]
            high_ref[comp, row] = turned[cols - 1]

            @pl.when(row == 0)
            def _():
                for col in range(cols):
                    first_ref[comp, :, pl.ds(col * depth, depth)] = turned[col]

        return carry

    lax.fori_loop(0, rows, body, 0, unroll=4)


def local_kernel(live_ref, coeff_ref, out_ref):
    comps, rows, count, width = live_ref.shape
    cols, depth = coeff_ref.shape[2:]
    lane = lax.broadcasted_iota(jnp.int32, (count, width), 1)
    last_z = (lane & (depth - 1)) == depth - 1

    def weight(entry, row):
        w = coeff_ref[entry, row]
        return jnp.concatenate([w[col:col + 1] for col in range(cols)], axis=1)

    def body(row, acc):
        has_next = row < rows - 1
        following_row = jnp.minimum(row + 1, rows - 1)
        w = [weight(e, row) for e in range(4)]
        lefts, rights = [], []
        for comp in range(comps):
            live = live_ref[comp, row]
            next_x = jnp.where(has_next, live_ref[comp, following_row], 0)
            next_y = jnp.concatenate([live[:, depth:], jnp.zeros_like(live[:, :depth])], axis=1)
            next_z = jnp.where(last_z, 0, pltpu.roll(live, width - 1, 1))
            step_x = live - next_x
            step_y = live - next_y
            step_z = live - next_z
            lefts += [live, step_x, step_y, step_z]
            rights += [w[0] * live, w[1] * step_x, w[2] * step_y, w[3] * step_z]
        left = jnp.concatenate(lefts, axis=1)
        right = jnp.concatenate(rights, axis=1)
        return acc + lax.dot_general(
            left, right, (((1,), (1,)), ((), ())), preferred_element_type=jnp.float32
        )

    out_ref[...] = lax.fori_loop(0, rows, body, jnp.zeros((count, count), jnp.float32), unroll=8)


def turned_field(deflation, depths):
    count, comps, rows, cols, depth = deflation.shape
    return pl.pallas_call(
        turn_kernel,
        out_shape=(
            jax.ShapeDtypeStruct((comps, rows, count, cols * depth), jnp.bfloat16),
            jax.ShapeDtypeStruct((comps, rows, count, depth), jnp.bfloat16),
            jax.ShapeDtypeStruct((comps, rows, count, depth), jnp.bfloat16),
            jax.ShapeDtypeStruct((comps, count, cols * depth), jnp.bfloat16),
        ),
        in_specs=[pl.BlockSpec(memory_space=pltpu.SMEM), pl.BlockSpec(memory_space=pltpu.VMEM)],
        out_specs=(pl.BlockSpec(memory_space=pltpu.VMEM),) * 4,
        cost_estimate=pl.CostEstimate(flops=0, bytes_accessed=deflation.size * 5, transcendentals=0),
    )(depths, deflation)


def local_terms(live_t, coefficients):
    count = live_t.shape[2]
    return pl.pallas_call(
        local_kernel,
        out_shape=jax.ShapeDtypeStruct((count, count), jnp.float32),
        in_specs=[pl.BlockSpec(memory_space=pltpu.VMEM)] * 2,
        out_specs=pl.BlockSpec(memory_space=pltpu.VMEM),
        cost_estimate=pl.CostEstimate(
            flops=2 * 4 * count * live_t.size,
            bytes_accessed=live_t.size * 2 + coefficients.size * 2,
            transcendentals=0,
        ),
    )(live_t, coefficients)


def face_gram(left_side, right_side):
    return jnp.einsum("cxkz,cxlz->kl", left_side, right_side, preferred_element_type=jnp.float32)


def layer_gram(left_side, right_side):
    return jnp.einsum("ckj,clj->kl", left_side, right_side, preferred_element_type=jnp.float32)


def shards(deflation, stiffness, depths):
    cell_count = deflation.shape[2] * deflation.shape[3] * deflation.shape[4]
    normalizer = 1.0 / (24.0 * cell_count)
    low_y, deflation = lax.optimization_barrier((low_layer(deflation, depths), deflation))
    next_y = from_behind(low_y, "grp", -1)
    live_t, bottom_y, top_y, bottom_x = turned_field(deflation, depths)
    weight_top_x = stiffness[1, -1].reshape(-1)
    weight_top_y = stiffness[2, :, -1]
    live_t, bottom_y, bottom_x, weight_top_x, weight_top_y = lax.optimization_barrier(
        (live_t, bottom_y, bottom_x, weight_top_x, weight_top_y)
    )
    next_x = from_behind(bottom_x, "sub", -1)
    weight_low_x = from_behind(weight_top_x, "sub", 1)
    weight_low_y = from_behind(weight_top_y, "grp", 1)
    diagonal_block = local_terms(live_t, stiffness)
    top_x = live_t[:, -1]
    coupling_x = -layer_gram(weighted(weight_top_x, top_x), next_x)
    coupling_y = -face_gram(weighted(weight_top_y[None, :, None], top_y), next_y)
    diagonal_block = diagonal_block + layer_gram(bottom_x, weighted(weight_low_x, bottom_x))
    diagonal_block = diagonal_block + face_gram(bottom_y, weighted(weight_low_y[None, :, None], bottom_y))
    row_block = normalizer * jnp.concatenate([diagonal_block, coupling_x, coupling_y], axis=1)
    groups = lax.axis_size("grp")
    dense = row_block.reshape(-1, 128)
    copies = jnp.broadcast_to(dense[None, None], (1, groups) + dense.shape)
    gathered = lax.all_to_all(copies, "grp", 1, 1, tiled=True)
    return gathered.reshape((1, groups) + row_block.shape)


def solution(mesh):
    in_specs = (P(None, None, "sub", "grp", None), P(None, "sub", "grp", None), P(("sub", "grp")))
    out_specs = P("sub", None, None, None)
    return jax.shard_map(shards, mesh=mesh, in_specs=in_specs, out_specs=out_specs, check_vma=False)
```

```python
import jax
import jax.numpy as jnp
from jax import lax
from jax.experimental import pallas as pl
from jax.experimental.pallas import tpu as pltpu
from jax.sharding import PartitionSpec as P


def from_behind(x, axis, by):
    length = lax.axis_size(axis)
    pairs = [(i, i + by) for i in range(length) if 0 <= i + by < length]
    return lax.ppermute(x, axis, pairs)


def gram_of(left_side, right_side):
    count = left_side.shape[0]
    return jnp.dot(
        left_side.reshape(count, -1),
        right_side.reshape(count, -1).T,
        preferred_element_type=jnp.float32,
    )


def weighted(weight, values):
    return (weight.astype(jnp.float32) * values.astype(jnp.float32)).astype(jnp.bfloat16)


def turn_kernel(depth_ref, defl_ref, live_ref, low_ref, high_ref, first_ref):
    count, comps, rows, cols, depth = defl_ref.shape
    lane = lax.broadcasted_iota(jnp.int32, (count, cols, depth), 2)
    live_mask = (lane < depth_ref[0]).astype(jnp.bfloat16)

    def body(row, carry):
        for comp in range(comps):
            tiles = (defl_ref[:, comp, row] * live_mask).astype(jnp.float32)
            turned = pltpu.einshape("kyz->ykz", tiles).astype(jnp.bfloat16)
            for col in range(cols):
                live_ref[comp, row, :, pl.ds(col * depth, depth)] = turned[col]
            low_ref[comp, row] = turned[0]
            high_ref[comp, row] = turned[cols - 1]

            @pl.when(row == 0)
            def _():
                for col in range(cols):
                    first_ref[comp, :, pl.ds(col * depth, depth)] = turned[col]

        return carry

    lax.fori_loop(0, rows, body, 0, unroll=4)


def local_kernel(live_ref, coeff_ref, out_ref):
    comps, rows, count, width = live_ref.shape
    cols, depth = coeff_ref.shape[2:]
    lane = lax.broadcasted_iota(jnp.int32, (count, width), 1)
    last_z = (lane & (depth - 1)) == depth - 1

    def weight(entry, row):
        w = coeff_ref[entry, row]
        return jnp.concatenate([w[col:col + 1] for col in range(cols)], axis=1)

    def body(row, acc):
        has_next = row < rows - 1
        following_row = jnp.minimum(row + 1, rows - 1)
        w = [weight(e, row) for e in range(4)]
        lefts, rights = [], []
        for comp in range(comps):
            live = live_ref[comp, row]
            next_x = jnp.where(has_next, live_ref[comp, following_row], 0)
            next_y = jnp.concatenate([live[:, depth:], jnp.zeros_like(live[:, :depth])], axis=1)
            next_z = jnp.where(last_z, 0, pltpu.roll(live, width - 1, 1))
            step_x = live - next_x
            step_y = live - next_y
            step_z = live - next_z
            lefts += [live, step_x, step_y, step_z]
            rights += [w[0] * live, w[1] * step_x, w[2] * step_y, w[3] * step_z]
        left = jnp.concatenate(lefts, axis=1)
        right = jnp.concatenate(rights, axis=1)
        return acc + lax.dot_general(
            left, right, (((1,), (1,)), ((), ())), preferred_element_type=jnp.float32
        )

    out_ref[...] = lax.fori_loop(0, rows, body, jnp.zeros((count, count), jnp.float32), unroll=8)


def turned_field(deflation, depths):
    count, comps, rows, cols, depth = deflation.shape
    return pl.pallas_call(
        turn_kernel,
        out_shape=(
            jax.ShapeDtypeStruct((comps, rows, count, cols * depth), jnp.bfloat16),
            jax.ShapeDtypeStruct((comps, rows, count, depth), jnp.bfloat16),
            jax.ShapeDtypeStruct((comps, rows, count, depth), jnp.bfloat16),
            jax.ShapeDtypeStruct((comps, count, cols * depth), jnp.bfloat16),
        ),
        in_specs=[pl.BlockSpec(memory_space=pltpu.SMEM), pl.BlockSpec(memory_space=pltpu.VMEM)],
        out_specs=(pl.BlockSpec(memory_space=pltpu.VMEM),) * 4,
        cost_estimate=pl.CostEstimate(flops=0, bytes_accessed=deflation.size * 5, transcendentals=0),
    )(depths, deflation)


def local_terms(live_t, coefficients):
    count = live_t.shape[2]
    return pl.pallas_call(
        local_kernel,
        out_shape=jax.ShapeDtypeStruct((count, count), jnp.float32),
        in_specs=[pl.BlockSpec(memory_space=pltpu.VMEM)] * 2,
        out_specs=pl.BlockSpec(memory_space=pltpu.VMEM),
        cost_estimate=pl.CostEstimate(
            flops=2 * 4 * count * live_t.size,
            bytes_accessed=live_t.size * 2 + coefficients.size * 2,
            transcendentals=0,
        ),
    )(live_t, coefficients)


def face_gram(left_side, right_side):
    return jnp.einsum("cxkz,cxlz->kl", left_side, right_side, preferred_element_type=jnp.float32)


def layer_gram(left_side, right_side):
    return jnp.einsum("ckj,clj->kl", left_side, right_side, preferred_element_type=jnp.float32)


def shards(deflation, stiffness, depths):
    cell_count = deflation.shape[2] * deflation.shape[3] * deflation.shape[4]
    normalizer = 1.0 / (24.0 * cell_count)
    live_t, bottom_y, top_y, bottom_x = turned_field(deflation, depths)
    weight_top_x = stiffness[1, -1].reshape(-1)
    weight_top_y = stiffness[2, :, -1]
    live_t, bottom_y, bottom_x, weight_top_x, weight_top_y = lax.optimization_barrier(
        (live_t, bottom_y, bottom_x, weight_top_x, weight_top_y)
    )
    next_y = from_behind(bottom_y, "grp", -1)
    next_x = from_behind(bottom_x, "sub", -1)
    weight_low_x = from_behind(weight_top_x, "sub", 1)
    diagonal_block = local_terms(live_t, stiffness)
    top_x = live_t[:, -1]
    coupling_x = -layer_gram(weighted(weight_top_x, top_x), next_x)
    coupling_y = -face_gram(weighted(weight_top_y[None, :, None], top_y), next_y)
    diagonal_block = diagonal_block + layer_gram(bottom_x, weighted(weight_low_x, bottom_x))
    lower_y_next = face_gram(next_y, weighted(weight_top_y[None, :, None], next_y))
    row_block = normalizer * jnp.concatenate([diagonal_block, coupling_x, coupling_y, lower_y_next], axis=1)
    groups = lax.axis_size("grp")
    count = diagonal_block.shape[0]
    copies = jnp.broadcast_to(row_block[None, None], (1, groups) + row_block.shape)
    gathered = lax.all_to_all(copies, "grp", 1, 1, tiled=True)
    from_below = jnp.pad(gathered[:, :-1, :, 3 * count:], ((0, 0), (1, 0), (0, 0), (0, 0)))
    return jnp.concatenate([gathered[..., :count] + from_below, gathered[..., count:3 * count]], axis=-1)


def solution(mesh):
    in_specs = (P(None, None, "sub", "grp", None), P(None, "sub", "grp", None), P(("sub", "grp")))
    out_specs = P("sub", None, None, None)
    return jax.shard_map(shards, mesh=mesh, in_specs=in_specs, out_specs=out_specs, check_vma=False)
```

```python
import jax
import jax.numpy as jnp
from jax import lax
from jax.experimental import pallas as pl
from jax.experimental.pallas import tpu as pltpu
from jax.sharding import PartitionSpec as P


def from_behind(x, axis, by):
    length = lax.axis_size(axis)
    pairs = [(i, i + by) for i in range(length) if 0 <= i + by < length]
    return lax.ppermute(x, axis, pairs)


def gram_of(left_side, right_side):
    count = left_side.shape[0]
    return jnp.dot(
        left_side.reshape(count, -1),
        right_side.reshape(count, -1).T,
        preferred_element_type=jnp.float32,
    )


def weighted(weight, values):
    return (weight.astype(jnp.float32) * values.astype(jnp.float32)).astype(jnp.bfloat16)


def turn_kernel(depth_ref, defl_ref, low_ref, high_ref, first_ref, last_ref):
    count, comps, rows, cols, depth = defl_ref.shape
    lane = lax.broadcasted_iota(jnp.int32, (count, cols, depth), 2)
    live_mask = (lane < depth_ref[0]).astype(jnp.bfloat16)

    def body(row, carry):
        for comp in range(comps):
            tiles = (defl_ref[:, comp, row] * live_mask).astype(jnp.float32)
            turned = pltpu.einshape("kyz->ykz", tiles).astype(jnp.bfloat16)
            low_ref[comp, row] = turned[0]
            high_ref[comp, row] = turned[cols - 1]

            @pl.when(row == 0)
            def _():
                for col in range(cols):
                    first_ref[comp, :, pl.ds(col * depth, depth)] = turned[col]

            @pl.when(row == rows - 1)
            def _():
                for col in range(cols):
                    last_ref[comp, :, pl.ds(col * depth, depth)] = turned[col]

        return carry

    lax.fori_loop(0, rows, body, 0, unroll=4)


def local_kernel(depth_ref, defl_ref, coeff_ref, out_ref):
    count, comps, rows, cols, depth = defl_ref.shape
    width = cols * depth
    lane = lax.broadcasted_iota(jnp.int32, (count, cols, depth), 2)
    live_mask = (lane < depth_ref[0]).astype(jnp.bfloat16)
    wide_lane = lax.broadcasted_iota(jnp.int32, (count, width), 1)
    last_z = (wide_lane & (depth - 1)) == depth - 1
    zero_slab = jnp.zeros((count, depth), jnp.float32)

    def flat(row, comp):
        tiles = (defl_ref[:, comp, row] * live_mask).astype(jnp.float32)
        turned = pltpu.einshape("kyz->ykz", tiles)
        return jnp.concatenate([turned[col] for col in range(cols)], axis=1).astype(jnp.bfloat16)

    def weight(entry, row):
        w = coeff_ref[entry, row]
        return jnp.concatenate([w[col:col + 1] for col in range(cols)], axis=1)

    def body(row, acc):
        has_next = row < rows - 1
        following_row = jnp.minimum(row + 1, rows - 1)
        w = [weight(e, row) for e in range(4)]
        lefts, rights = [], []
        for comp in range(comps):
            live = flat(row, comp)
            next_x = jnp.where(has_next, flat(following_row, comp), 0)
            next_y = jnp.concatenate([live[:, depth:], jnp.zeros_like(live[:, :depth])], axis=1)
            next_z = jnp.where(last_z, 0, pltpu.roll(live, width - 1, 1))
            step_x = live - next_x
            step_y = live - next_y
            step_z = live - next_z
            lefts += [live, step_x, step_y, step_z]
            rights += [w[0] * live, w[1] * step_x, w[2] * step_y, w[3] * step_z]
        left = jnp.concatenate(lefts, axis=1)
        right = jnp.concatenate(rights, axis=1)
        return acc + lax.dot_general(
            left, right, (((1,), (1,)), ((), ())), preferred_element_type=jnp.float32
        )

    out_ref[...] = lax.fori_loop(0, rows, body, jnp.zeros((count, count), jnp.float32), unroll=8)


def turned_field(deflation, depths):
    count, comps, rows, cols, depth = deflation.shape
    return pl.pallas_call(
        turn_kernel,
        out_shape=(
            jax.ShapeDtypeStruct((comps, rows, count, depth), jnp.bfloat16),
            jax.ShapeDtypeStruct((comps, rows, count, depth), jnp.bfloat16),
            jax.ShapeDtypeStruct((comps, count, cols * depth), jnp.bfloat16),
            jax.ShapeDtypeStruct((comps, count, cols * depth), jnp.bfloat16),
        ),
        in_specs=[pl.BlockSpec(memory_space=pltpu.SMEM), pl.BlockSpec(memory_space=pltpu.VMEM)],
        out_specs=(pl.BlockSpec(memory_space=pltpu.VMEM),) * 4,
        cost_estimate=pl.CostEstimate(flops=0, bytes_accessed=deflation.size * 3, transcendentals=0),
    )(depths, deflation)


def local_terms(deflation, coefficients, depths):
    count = deflation.shape[0]
    return pl.pallas_call(
        local_kernel,
        out_shape=jax.ShapeDtypeStruct((count, count), jnp.float32),
        in_specs=[pl.BlockSpec(memory_space=pltpu.SMEM)] + [pl.BlockSpec(memory_space=pltpu.VMEM)] * 2,
        out_specs=pl.BlockSpec(memory_space=pltpu.VMEM),
        cost_estimate=pl.CostEstimate(
            flops=2 * 4 * count * deflation.size,
            bytes_accessed=deflation.size * 2 + coefficients.size * 2,
            transcendentals=0,
        ),
    )(depths, deflation, coefficients)


def face_gram(left_side, right_side):
    return jnp.einsum("cxkz,cxlz->kl", left_side, right_side, preferred_element_type=jnp.float32)


def layer_gram(left_side, right_side):
    return jnp.einsum("ckj,clj->kl", left_side, right_side, preferred_element_type=jnp.float32)


def shards(deflation, stiffness, depths):
    cell_count = deflation.shape[2] * deflation.shape[3] * deflation.shape[4]
    normalizer = 1.0 / (24.0 * cell_count)
    bottom_y, top_y, bottom_x, top_x = turned_field(deflation, depths)
    weight_top_x = stiffness[1, -1].reshape(-1)
    weight_top_y = stiffness[2, :, -1]
    bottom_y, bottom_x, weight_top_x, weight_top_y = lax.optimization_barrier(
        (bottom_y, bottom_x, weight_top_x, weight_top_y)
    )
    next_y = from_behind(bottom_y, "grp", -1)
    next_x = from_behind(bottom_x, "sub", -1)
    weight_low_x = from_behind(weight_top_x, "sub", 1)
    diagonal_block = local_terms(deflation, stiffness, depths)
    coupling_x = -layer_gram(weighted(weight_top_x, top_x), next_x)
    coupling_y = -face_gram(weighted(weight_top_y[None, :, None], top_y), next_y)
    diagonal_block = diagonal_block + layer_gram(bottom_x, weighted(weight_low_x, bottom_x))
    lower_y_next = face_gram(next_y, weighted(weight_top_y[None, :, None], next_y))
    row_block = normalizer * jnp.concatenate([diagonal_block, coupling_x, coupling_y, lower_y_next], axis=1)
    groups = lax.axis_size("grp")
    count = diagonal_block.shape[0]
    copies = jnp.broadcast_to(row_block[None, None], (1, groups) + row_block.shape)
    gathered = lax.all_to_all(copies, "grp", 1, 1, tiled=True)
    from_below = jnp.pad(gathered[:, :-1, :, 3 * count:], ((0, 0), (1, 0), (0, 0), (0, 0)))
    return jnp.concatenate([gathered[..., :count] + from_below, gathered[..., count:3 * count]], axis=-1)


def solution(mesh):
    in_specs = (P(None, None, "sub", "grp", None), P(None, "sub", "grp", None), P(("sub", "grp")))
    out_specs = P("sub", None, None, None)
    return jax.shard_map(shards, mesh=mesh, in_specs=in_specs, out_specs=out_specs, check_vma=False)
```

```python
import jax
import jax.numpy as jnp
from jax import lax
from jax.experimental import pallas as pl
from jax.experimental.pallas import tpu as pltpu
from jax.sharding import PartitionSpec as P


def from_behind(x, axis, by):
    length = lax.axis_size(axis)
    pairs = [(i, i + by) for i in range(length) if 0 <= i + by < length]
    return lax.ppermute(x, axis, pairs)


def gram_of(left_side, right_side):
    count = left_side.shape[0]
    return jnp.dot(
        left_side.reshape(count, -1),
        right_side.reshape(count, -1).T,
        preferred_element_type=jnp.float32,
    )


def weighted(weight, values):
    return (weight.astype(jnp.float32) * values.astype(jnp.float32)).astype(jnp.bfloat16)


def turn_kernel(depth_ref, defl_ref, low_ref, high_ref, first_ref, last_ref):
    count, comps, rows, cols, depth = defl_ref.shape
    lane = lax.broadcasted_iota(jnp.int32, (count, cols, depth), 2)
    live_mask = (lane < depth_ref[0]).astype(jnp.bfloat16)

    def body(row, carry):
        for comp in range(comps):
            tiles = (defl_ref[:, comp, row] * live_mask).astype(jnp.float32)
            turned = pltpu.einshape("kyz->ykz", tiles).astype(jnp.bfloat16)
            low_ref[comp, row] = turned[0]
            high_ref[comp, row] = turned[cols - 1]

            @pl.when(row == 0)
            def _():
                for col in range(cols):
                    first_ref[comp, :, pl.ds(col * depth, depth)] = turned[col]

            @pl.when(row == rows - 1)
            def _():
                for col in range(cols):
                    last_ref[comp, :, pl.ds(col * depth, depth)] = turned[col]

        return carry

    lax.fori_loop(0, rows, body, 0, unroll=4)


def local_kernel(depth_ref, defl_ref, coeff_ref, out_ref):
    count, comps, rows, cols, depth = defl_ref.shape
    width = cols * depth
    lane = lax.broadcasted_iota(jnp.int32, (count, cols, depth), 2)
    live_mask = (lane < depth_ref[0]).astype(jnp.bfloat16)
    wide_lane = lax.broadcasted_iota(jnp.int32, (count, width), 1)
    last_z = (wide_lane & (depth - 1)) == depth - 1
    zero_slab = jnp.zeros((count, depth), jnp.float32)

    def flat(row, comp):
        tiles = (defl_ref[:, comp, row] * live_mask).astype(jnp.float32)
        turned = pltpu.einshape("kyz->ykz", tiles)
        return jnp.concatenate([turned[col] for col in range(cols)], axis=1).astype(jnp.bfloat16)

    def weight(entry, row):
        w = coeff_ref[entry, row]
        return jnp.concatenate([w[col:col + 1] for col in range(cols)], axis=1)

    def body(row, acc):
        has_next = row < rows - 1
        following_row = jnp.minimum(row + 1, rows - 1)
        w = [weight(e, row) for e in range(4)]
        lefts, rights = [], []
        for comp in range(comps):
            live = flat(row, comp)
            next_x = jnp.where(has_next, flat(following_row, comp), 0)
            next_y = jnp.concatenate([live[:, depth:], jnp.zeros_like(live[:, :depth])], axis=1)
            next_z = jnp.where(last_z, 0, pltpu.roll(live, width - 1, 1))
            step_x = live - next_x
            step_y = live - next_y
            step_z = live - next_z
            lefts += [live, step_x, step_y, step_z]
            rights += [w[0] * live, w[1] * step_x, w[2] * step_y, w[3] * step_z]
        left = jnp.concatenate(lefts, axis=1)
        right = jnp.concatenate(rights, axis=1)
        return acc + lax.dot_general(
            left, right, (((1,), (1,)), ((), ())), preferred_element_type=jnp.float32
        )

    out_ref[...] = lax.fori_loop(0, rows, body, jnp.zeros((count, count), jnp.float32), unroll=8)


def turned_field(deflation, depths):
    count, comps, rows, cols, depth = deflation.shape
    return pl.pallas_call(
        turn_kernel,
        out_shape=(
            jax.ShapeDtypeStruct((comps, rows, count, depth), jnp.bfloat16),
            jax.ShapeDtypeStruct((comps, rows, count, depth), jnp.bfloat16),
            jax.ShapeDtypeStruct((comps, count, cols * depth), jnp.bfloat16),
            jax.ShapeDtypeStruct((comps, count, cols * depth), jnp.bfloat16),
        ),
        in_specs=[pl.BlockSpec(memory_space=pltpu.SMEM), pl.BlockSpec(memory_space=pltpu.VMEM)],
        out_specs=(pl.BlockSpec(memory_space=pltpu.VMEM),) * 4,
        cost_estimate=pl.CostEstimate(flops=0, bytes_accessed=deflation.size * 3, transcendentals=0),
    )(depths, deflation)


def local_terms(deflation, coefficients, depths):
    count = deflation.shape[0]
    return pl.pallas_call(
        local_kernel,
        out_shape=jax.ShapeDtypeStruct((count, count), jnp.float32),
        in_specs=[pl.BlockSpec(memory_space=pltpu.SMEM)] + [pl.BlockSpec(memory_space=pltpu.VMEM)] * 2,
        out_specs=pl.BlockSpec(memory_space=pltpu.VMEM),
        cost_estimate=pl.CostEstimate(
            flops=2 * 4 * count * deflation.size,
            bytes_accessed=deflation.size * 2 + coefficients.size * 2,
            transcendentals=0,
        ),
    )(depths, deflation, coefficients)


def face_gram(left_side, right_side):
    return jnp.einsum("cxkz,cxlz->kl", left_side, right_side, preferred_element_type=jnp.float32)


def layer_gram(left_side, right_side):
    return jnp.einsum("ckj,clj->kl", left_side, right_side, preferred_element_type=jnp.float32)


def shards(deflation, stiffness, depths):
    cell_count = deflation.shape[2] * deflation.shape[3] * deflation.shape[4]
    normalizer = 1.0 / (24.0 * cell_count)
    bottom_y, top_y, bottom_x, top_x = turned_field(deflation, depths)
    weight_top_x = stiffness[1, -1].reshape(-1)
    weight_top_y = stiffness[2, :, -1]
    bottom_y, bottom_x, weight_top_y = lax.optimization_barrier((bottom_y, bottom_x, weight_top_y))
    next_y = from_behind(bottom_y, "grp", -1)
    next_x = from_behind(bottom_x, "sub", -1)
    weight_low_x = from_behind(weight_top_x, "sub", 1)
    diagonal_block = local_terms(deflation, stiffness, depths)
    coupling_x = -layer_gram(weighted(weight_top_x, top_x), next_x)
    coupling_y = -face_gram(weighted(weight_top_y[None, :, None], top_y), next_y)
    diagonal_block = diagonal_block + layer_gram(bottom_x, weighted(weight_low_x, bottom_x))
    lower_y_next = face_gram(next_y, weighted(weight_top_y[None, :, None], next_y))
    row_block = normalizer * jnp.concatenate([diagonal_block, coupling_x, coupling_y, lower_y_next], axis=1)
    groups = lax.axis_size("grp")
    count = diagonal_block.shape[0]
    copies = jnp.broadcast_to(row_block[None, None], (1, groups) + row_block.shape)
    gathered = lax.all_to_all(copies, "grp", 1, 1, tiled=True)
    from_below = jnp.pad(gathered[:, :-1, :, 3 * count:], ((0, 0), (1, 0), (0, 0), (0, 0)))
    return jnp.concatenate([gathered[..., :count] + from_below, gathered[..., count:3 * count]], axis=-1)


def solution(mesh):
    in_specs = (P(None, None, "sub", "grp", None), P(None, "sub", "grp", None), P(("sub", "grp")))
    out_specs = P("sub", None, None, None)
    return jax.shard_map(shards, mesh=mesh, in_specs=in_specs, out_specs=out_specs, check_vma=False)
```

```python
import jax
import jax.numpy as jnp
from jax import lax
from jax.experimental import pallas as pl
from jax.experimental.pallas import tpu as pltpu
from jax.sharding import PartitionSpec as P


def from_behind(x, axis, by):
    length = lax.axis_size(axis)
    pairs = [(i, i + by) for i in range(length) if 0 <= i + by < length]
    return lax.ppermute(x, axis, pairs)


def gram_of(left_side, right_side):
    count = left_side.shape[0]
    return jnp.dot(
        left_side.reshape(count, -1),
        right_side.reshape(count, -1).T,
        preferred_element_type=jnp.float32,
    )


def weighted(weight, values):
    return (weight.astype(jnp.float32) * values.astype(jnp.float32)).astype(jnp.bfloat16)


def turn_kernel(depth_ref, defl_ref, live_ref, low_ref, high_ref, first_ref):
    count, comps, rows, cols, depth = defl_ref.shape
    lane = lax.broadcasted_iota(jnp.int32, (count, cols, depth), 2)
    live_mask = (lane < depth_ref[0]).astype(jnp.bfloat16)

    def body(row, carry):
        for comp in range(comps):
            tiles = (defl_ref[:, comp, row] * live_mask).astype(jnp.float32)
            turned = pltpu.einshape("kyz->ykz", tiles).astype(jnp.bfloat16)
            for col in range(cols):
                live_ref[comp, row, :, pl.ds(col * depth, depth)] = turned[col]
            low_ref[comp, row] = turned[0]
            high_ref[comp, row] = turned[cols - 1]

            @pl.when(row == 0)
            def _():
                for col in range(cols):
                    first_ref[comp, :, pl.ds(col * depth, depth)] = turned[col]

        return carry

    lax.fori_loop(0, rows, body, 0, unroll=rows)


def local_kernel(live_ref, coeff_ref, out_ref):
    comps, rows, count, width = live_ref.shape
    cols, depth = coeff_ref.shape[2:]
    lane = lax.broadcasted_iota(jnp.int32, (count, width), 1)
    last_z = (lane & (depth - 1)) == depth - 1

    def weight(entry, row):
        w = coeff_ref[entry, row]
        return jnp.concatenate([w[col:col + 1] for col in range(cols)], axis=1)

    def body(row, acc):
        has_next = row < rows - 1
        following_row = jnp.minimum(row + 1, rows - 1)
        w = [weight(e, row) for e in range(4)]
        lefts, rights = [], []
        for comp in range(comps):
            live = live_ref[comp, row]
            next_x = jnp.where(has_next, live_ref[comp, following_row], 0)
            next_y = jnp.concatenate([live[:, depth:], jnp.zeros_like(live[:, :depth])], axis=1)
            next_z = jnp.where(last_z, 0, pltpu.roll(live, width - 1, 1))
            step_x = live - next_x
            step_y = live - next_y
            step_z = live - next_z
            lefts += [live, step_x, step_y, step_z]
            rights += [w[0] * live, w[1] * step_x, w[2] * step_y, w[3] * step_z]
        left = jnp.concatenate(lefts, axis=1)
        right = jnp.concatenate(rights, axis=1)
        return acc + lax.dot_general(
            left, right, (((1,), (1,)), ((), ())), preferred_element_type=jnp.float32
        )

    out_ref[...] = lax.fori_loop(0, rows, body, jnp.zeros((count, count), jnp.float32), unroll=rows)


def turned_field(deflation, depths):
    count, comps, rows, cols, depth = deflation.shape
    return pl.pallas_call(
        turn_kernel,
        out_shape=(
            jax.ShapeDtypeStruct((comps, rows, count, cols * depth), jnp.bfloat16),
            jax.ShapeDtypeStruct((comps, rows, count, depth), jnp.bfloat16),
            jax.ShapeDtypeStruct((comps, rows, count, depth), jnp.bfloat16),
            jax.ShapeDtypeStruct((comps, count, cols * depth), jnp.bfloat16),
        ),
        in_specs=[pl.BlockSpec(memory_space=pltpu.SMEM), pl.BlockSpec(memory_space=pltpu.VMEM)],
        out_specs=(pl.BlockSpec(memory_space=pltpu.VMEM),) * 4,
        cost_estimate=pl.CostEstimate(flops=0, bytes_accessed=deflation.size * 5, transcendentals=0),
    )(depths, deflation)


def local_terms(live_t, coefficients):
    count = live_t.shape[2]
    return pl.pallas_call(
        local_kernel,
        out_shape=jax.ShapeDtypeStruct((count, count), jnp.float32),
        in_specs=[pl.BlockSpec(memory_space=pltpu.VMEM)] * 2,
        out_specs=pl.BlockSpec(memory_space=pltpu.VMEM),
        cost_estimate=pl.CostEstimate(
            flops=2 * 4 * count * live_t.size,
            bytes_accessed=live_t.size * 2 + coefficients.size * 2,
            transcendentals=0,
        ),
    )(live_t, coefficients)


def face_gram(left_side, right_side):
    return jnp.einsum("cxkz,cxlz->kl", left_side, right_side, preferred_element_type=jnp.float32)


def layer_gram(left_side, right_side):
    return jnp.einsum("ckj,clj->kl", left_side, right_side, preferred_element_type=jnp.float32)


def shards(deflation, stiffness, depths):
    cell_count = deflation.shape[2] * deflation.shape[3] * deflation.shape[4]
    normalizer = 1.0 / (24.0 * cell_count)
    live_t, bottom_y, top_y, bottom_x = turned_field(deflation, depths)
    weight_top_x = stiffness[1, -1].reshape(-1)
    weight_top_y = stiffness[2, :, -1]
    live_t, bottom_y, bottom_x, weight_top_x, weight_top_y = lax.optimization_barrier(
        (live_t, bottom_y, bottom_x, weight_top_x, weight_top_y)
    )
    next_y = from_behind(bottom_y, "grp", -1)
    next_x = from_behind(bottom_x, "sub", -1)
    weight_low_x = from_behind(weight_top_x, "sub", 1)
    diagonal_block = local_terms(live_t, stiffness)
    top_x = live_t[:, -1]
    coupling_x = -layer_gram(weighted(weight_top_x, top_x), next_x)
    coupling_y = -face_gram(weighted(weight_top_y[None, :, None], top_y), next_y)
    diagonal_block = diagonal_block + layer_gram(bottom_x, weighted(weight_low_x, bottom_x))
    lower_y_next = face_gram(next_y, weighted(weight_top_y[None, :, None], next_y))
    row_block = normalizer * jnp.concatenate([diagonal_block, coupling_x, coupling_y, lower_y_next], axis=1)
    groups = lax.axis_size("grp")
    count = diagonal_block.shape[0]
    copies = jnp.broadcast_to(row_block[None, None], (1, groups) + row_block.shape)
    gathered = lax.all_to_all(copies, "grp", 1, 1, tiled=True)
    from_below = jnp.pad(gathered[:, :-1, :, 3 * count:], ((0, 0), (1, 0), (0, 0), (0, 0)))
    return jnp.concatenate([gathered[..., :count] + from_below, gathered[..., count:3 * count]], axis=-1)


def solution(mesh):
    in_specs = (P(None, None, "sub", "grp", None), P(None, "sub", "grp", None), P(("sub", "grp")))
    out_specs = P("sub", None, None, None)
    return jax.shard_map(shards, mesh=mesh, in_specs=in_specs, out_specs=out_specs, check_vma=False)
```

```python
import jax
import jax.numpy as jnp
from jax import lax
from jax.experimental import pallas as pl
from jax.experimental.pallas import tpu as pltpu
from jax.sharding import PartitionSpec as P


def from_behind(x, axis, by):
    length = lax.axis_size(axis)
    pairs = [(i, i + by) for i in range(length) if 0 <= i + by < length]
    return lax.ppermute(x, axis, pairs)


def gram_of(left_side, right_side):
    count = left_side.shape[0]
    return jnp.dot(
        left_side.reshape(count, -1),
        right_side.reshape(count, -1).T,
        preferred_element_type=jnp.float32,
    )


def weighted(weight, values):
    return (weight.astype(jnp.float32) * values.astype(jnp.float32)).astype(jnp.bfloat16)


def turn_kernel(depth_ref, defl_ref, live_ref, low_ref, high_ref, first_ref):
    count, comps, rows, cols, depth = defl_ref.shape
    lane = lax.broadcasted_iota(jnp.int32, (count, cols, depth), 2)
    live_mask = (lane < depth_ref[0]).astype(jnp.bfloat16)

    def body(row, carry):
        for comp in range(comps):
            turned = pltpu.einshape("kyz->ykz", defl_ref[:, comp, row] * live_mask)
            for col in range(cols):
                live_ref[comp, row, :, pl.ds(col * depth, depth)] = turned[col]
            low_ref[comp, row] = turned[0]
            high_ref[comp, row] = turned[cols - 1]

            @pl.when(row == 0)
            def _():
                for col in range(cols):
                    first_ref[comp, :, pl.ds(col * depth, depth)] = turned[col]

        return carry

    lax.fori_loop(0, rows, body, 0, unroll=rows)


def local_kernel(live_ref, coeff_ref, out_ref):
    comps, rows, count, width = live_ref.shape
    cols, depth = coeff_ref.shape[2:]
    lane = lax.broadcasted_iota(jnp.int32, (count, width), 1)
    last_z = (lane & (depth - 1)) == depth - 1

    def weight(entry, row):
        w = coeff_ref[entry, row]
        return jnp.concatenate([w[col:col + 1] for col in range(cols)], axis=1)

    def body(row, acc):
        has_next = row < rows - 1
        following_row = jnp.minimum(row + 1, rows - 1)
        w = [weight(e, row) for e in range(4)]
        lefts, rights = [], []
        for comp in range(comps):
            live = live_ref[comp, row]
            next_x = jnp.where(has_next, live_ref[comp, following_row], 0)
            next_y = jnp.concatenate([live[:, depth:], jnp.zeros_like(live[:, :depth])], axis=1)
            next_z = jnp.where(last_z, 0, pltpu.roll(live, width - 1, 1))
            step_x = live - next_x
            step_y = live - next_y
            step_z = live - next_z
            lefts += [live, step_x, step_y, step_z]
            rights += [w[0] * live, w[1] * step_x, w[2] * step_y, w[3] * step_z]
        left = jnp.concatenate(lefts, axis=1)
        right = jnp.concatenate(rights, axis=1)
        return acc + lax.dot_general(
            left, right, (((1,), (1,)), ((), ())), preferred_element_type=jnp.float32
        )

    out_ref[...] = lax.fori_loop(0, rows, body, jnp.zeros((count, count), jnp.float32), unroll=rows)


def turned_field(deflation, depths):
    count, comps, rows, cols, depth = deflation.shape
    return pl.pallas_call(
        turn_kernel,
        out_shape=(
            jax.ShapeDtypeStruct((comps, rows, count, cols * depth), jnp.bfloat16),
            jax.ShapeDtypeStruct((comps, rows, count, depth), jnp.bfloat16),
            jax.ShapeDtypeStruct((comps, rows, count, depth), jnp.bfloat16),
            jax.ShapeDtypeStruct((comps, count, cols * depth), jnp.bfloat16),
        ),
        in_specs=[pl.BlockSpec(memory_space=pltpu.SMEM), pl.BlockSpec(memory_space=pltpu.VMEM)],
        out_specs=(pl.BlockSpec(memory_space=pltpu.VMEM),) * 4,
        cost_estimate=pl.CostEstimate(flops=0, bytes_accessed=deflation.size * 5, transcendentals=0),
    )(depths, deflation)


def local_terms(live_t, coefficients):
    count = live_t.shape[2]
    return pl.pallas_call(
        local_kernel,
        out_shape=jax.ShapeDtypeStruct((count, count), jnp.float32),
        in_specs=[pl.BlockSpec(memory_space=pltpu.VMEM)] * 2,
        out_specs=pl.BlockSpec(memory_space=pltpu.VMEM),
        cost_estimate=pl.CostEstimate(
            flops=2 * 4 * count * live_t.size,
            bytes_accessed=live_t.size * 2 + coefficients.size * 2,
            transcendentals=0,
        ),
    )(live_t, coefficients)


def face_gram(left_side, right_side):
    return jnp.einsum("cxkz,cxlz->kl", left_side, right_side, preferred_element_type=jnp.float32)


def layer_gram(left_side, right_side):
    return jnp.einsum("ckj,clj->kl", left_side, right_side, preferred_element_type=jnp.float32)


def shards(deflation, stiffness, depths):
    cell_count = deflation.shape[2] * deflation.shape[3] * deflation.shape[4]
    normalizer = 1.0 / (24.0 * cell_count)
    live_t, bottom_y, top_y, bottom_x = turned_field(deflation, depths)
    weight_top_x = stiffness[1, -1].reshape(-1)
    weight_top_y = stiffness[2, :, -1]
    live_t, bottom_y, bottom_x, weight_top_x, weight_top_y = lax.optimization_barrier(
        (live_t, bottom_y, bottom_x, weight_top_x, weight_top_y)
    )
    next_y = from_behind(bottom_y, "grp", -1)
    next_x = from_behind(bottom_x, "sub", -1)
    weight_low_x = from_behind(weight_top_x, "sub", 1)
    diagonal_block = local_terms(live_t, stiffness)
    top_x = live_t[:, -1]
    coupling_x = -layer_gram(weighted(weight_top_x, top_x), next_x)
    coupling_y = -face_gram(weighted(weight_top_y[None, :, None], top_y), next_y)
    diagonal_block = diagonal_block + layer_gram(bottom_x, weighted(weight_low_x, bottom_x))
    lower_y_next = face_gram(next_y, weighted(weight_top_y[None, :, None], next_y))
    row_block = normalizer * jnp.concatenate([diagonal_block, coupling_x, coupling_y, lower_y_next], axis=1)
    groups = lax.axis_size("grp")
    count = diagonal_block.shape[0]
    copies = jnp.broadcast_to(row_block[None, None], (1, groups) + row_block.shape)
    gathered = lax.all_to_all(copies, "grp", 1, 1, tiled=True)
    from_below = jnp.pad(gathered[:, :-1, :, 3 * count:], ((0, 0), (1, 0), (0, 0), (0, 0)))
    return jnp.concatenate([gathered[..., :count] + from_below, gathered[..., count:3 * count]], axis=-1)


def solution(mesh):
    in_specs = (P(None, None, "sub", "grp", None), P(None, "sub", "grp", None), P(("sub", "grp")))
    out_specs = P("sub", None, None, None)
    return jax.shard_map(shards, mesh=mesh, in_specs=in_specs, out_specs=out_specs, check_vma=False)
```
